256 devices in a mesh: pair: 2 (over core), seq: 32 (over y, x, z_hi), tp: 4 (over z_lo).
Axes of the slice: x: 4, y: 4, z: 8 (z_hi: 2, z_lo: 4; z = z_hi * 4 + z_lo), core: 2. Of those that a mesh axis runs over, the one named last changes fastest.
Arguments:
- hidden: bfloat16 [36864, 3072], P(('pair', 'seq'), 'tp'), may hold values from -11 to 11
- positions: int32 [3, 36864], P(None, ('pair', 'seq')), may hold values from 0 to 63, as said below
- lengths: int32 [8], P('pair'), may hold values from 1 to 512, as said below
- step_index: int32 [1], replicated, may hold values from 0 to 7
- layer_mod: float32 [8, 3, 3072], P('pair'), may hold values from -3 to 3
- final_mod: float32 [8, 2, 3072], P('pair'), may hold values from -3 to 3
- qkv_weight: bfloat16 [3072, 3, 1536], P(None, None, 'tp'), may hold values from -0.108253175 to 0.108253175
- q_gain: float32 [128], replicated, may hold values from 0.5 to 5.5
- k_gain: float32 [128], replicated, may hold values from 0.5 to 5.5
- out_weight: bfloat16 [1536, 3072], P('tp'), may hold values from -0.15625 to 0.15625
- final_weight: bfloat16 [3072, 64], P('tp'), may hold values from -0.109375 to 0.109375
- latents: float32 [16384, 64], P(('pair', 'seq')), may hold values from -6 to 6
Outputs:
- new_hidden: bfloat16 [36864, 3072], P(('pair', 'seq'), 'tp')
- attention_lse: float32 [12, 36864], P('tp', ('pair', 'seq'))
- next_latents: float32 [16384, 64], P(('pair', 'seq'))
The draws below stay inside these ranges and needn't reach their ends.
Inputs may be any that keep to these rules, and one draw needn't show every extreme that they name: `lengths`: some sequence has all 512 text tokens live and some sequence just one. `positions`: the first component is zero; text rows are zero; the image rows of a sequence hold each cell (row, column) of a grid 64 cells wide exactly once, the same for both sequences of a prompt.
All inputs are finite; a program needn't handle non-finite values.
Results may differ from the reference program's by a relative error of at most 0.01.
Values may be sent and summed in bfloat16 or wider, within the bound.
No kernel may reach another device: no remote copies, remote signals or barrier semaphores. Data moves between devices by JAX's collectives and lax.ppermute only.
A program may use at most 128 MiB of HBM per device.

```python
import math
import jax
import jax.numpy as jnp
from jax import lax

D = 3072
HEADS = 12
ROPE_T = 16
ROPE_H = 56
ROPE_W = 56
HEAD_DIM = 128
CH = 64
WID = 64
STEPS = 8
IMG_DEV = 512
TXT_DEV = 64
S = 8
IMG = 4096
TXT = 512
L = 4608
ROWS_DEV = 576
HALF = 256
SEQS = 8
PROMPTS = 4
ROWS = 36864


def draw_hidden(key, part):
    draw_key = jax.random.fold_in(key, 41)
    channel_scale = 0.6 + 1.2 * jnp.arange(D, dtype=jnp.float32) / D
    result = jax.random.normal(draw_key, (ROWS, D), jnp.float32) * channel_scale
    return jnp.clip(result, -11.0, 11.0).astype(jnp.bfloat16)


def draw_positions(key, part):
    prompts = SEQS // 2
    shards = IMG // IMG_DEV
    draw_key = jax.random.fold_in(key, 21)
    grid_cells = jax.vmap(lambda subkey: jax.random.permutation(subkey, IMG))(jax.random.split(draw_key, prompts))
    grid_cells = jnp.broadcast_to(grid_cells[:, None, :], (prompts, 2, IMG)).reshape(prompts, 2, shards, IMG_DEV).astype(jnp.int32)
    text_zero = jnp.zeros((prompts, 2, shards, TXT_DEV), jnp.int32)
    grid_row = jnp.concatenate([grid_cells // WID, text_zero], axis=3).reshape(ROWS)
    grid_col = jnp.concatenate([grid_cells % WID, text_zero], axis=3).reshape(ROWS)
    return jnp.stack([jnp.zeros((ROWS,), jnp.int32), grid_row, grid_col]).astype(jnp.int32)


def draw_lengths(key, part):
    text_counts = jax.random.randint(jax.random.fold_in(key, 31), (SEQS,), 1, TXT + 1).astype(jnp.int32)
    return text_counts.at[0].set(TXT).at[1].set(1)


def gain_common(key, first_tag):
    spread_vals = jax.random.uniform(jax.random.fold_in(key, first_tag), (HEAD_DIM,), jnp.float32)
    result = 0.5 * jnp.exp(spread_vals * math.log(4.0))
    return jnp.clip(result, 0.5, 5.5)


def draw_q_gain(key, part):
    return gain_common(key, 51)


def draw_k_gain(key, part):
    return gain_common(key, 53)


def draw_qkv_weight(key, part):
    base_vals = jax.random.normal(jax.random.fold_in(key, 61), (D, 3, HEADS * HEAD_DIM), jnp.float32)
    result = base_vals
    return (jnp.clip(result, -6.0, 6.0) * D ** (-0.5)).astype(jnp.bfloat16)


def block_scale(key, shape, cuts, low, high):
    def one(position, shards_of):
        steps = jax.random.uniform(jax.random.fold_in(jax.random.fold_in(key, 6), position), (shards_of,), jnp.float32, low / len(cuts), high / len(cuts))
        return jnp.repeat(jnp.exp(steps), shape[position] // shards_of).reshape((-1,) + (1,) * (len(shape) - position - 1))

    gain = one(*cuts[0])
    for cut in cuts[1:]:
        gain = gain * one(*cut)
    return gain


def scatter_about(stream_key, shape, scale, most, cuts=(), kind=jnp.bfloat16):
    values = scale * jax.random.normal(stream_key, shape, jnp.float32)
    if cuts:
        values = values * block_scale(stream_key, shape, cuts, -0.22, 0.18)
    return jnp.clip(values, -most, most).astype(kind)


def setup_inputs(seed: int = 0) -> dict:
    keys = jax.random.split(jax.random.key(seed), 13)
    hidden = draw_hidden(jax.random.fold_in(keys[12], 71), 0)
    positions = draw_positions(jax.random.fold_in(keys[12], 71), 0)
    lengths = draw_lengths(jax.random.fold_in(keys[12], 71), 0)
    step_index = jax.random.randint(keys[3], (1,), 0, STEPS).astype(jnp.int32)
    layer_mod = scatter_about(keys[4], (SEQS, 3, D), 0.5, 3.0, ((0, 2),), jnp.float32)
    final_mod = scatter_about(keys[5], (SEQS, 2, D), 0.5, 3.0, ((0, 2),), jnp.float32)
    qkv_weight = draw_qkv_weight(jax.random.fold_in(keys[12], 71), 0)
    q_gain = draw_q_gain(jax.random.fold_in(keys[12], 71), 0)
    k_gain = draw_k_gain(jax.random.fold_in(keys[12], 71), 0)
    out_weight = scatter_about(keys[9], (HEADS * HEAD_DIM, D), (HEADS * HEAD_DIM) ** -0.5, 0.15625, ((0, 4),))
    final_weight = scatter_about(keys[10], (D, CH), D ** -0.5, 0.109375, ((0, 4),))
    latents = scatter_about(keys[11], (PROMPTS * IMG, CH), 1.0, 6.0, ((0, 64),), jnp.float32)
    return dict(hidden=hidden, positions=positions, lengths=lengths, step_index=step_index, layer_mod=layer_mod, final_mod=final_mod, qkv_weight=qkv_weight, q_gain=q_gain, k_gain=k_gain, out_weight=out_weight, final_weight=final_weight, latents=latents)


GUIDE = 3.5
SHIFT = 3.0

def rope_angles(ids_block):
    angle_parts = []
    for axis_pos, rope_width in ((0, ROPE_T), (1, ROPE_H), (2, ROPE_W)):
        frequencies = 10000.0 ** (-jnp.arange(0, rope_width, 2).astype(jnp.float32) / rope_width)
        angle_parts.append(ids_block[axis_pos].astype(jnp.float32)[:, None] * frequencies[None, :])
    angles = jnp.concatenate(angle_parts, axis=1)
    return (jnp.cos(angles), jnp.sin(angles))

def rotate(tensor, cosine, sine_part):
    dims_in = tensor.shape
    pair_view = tensor.reshape(dims_in[0], dims_in[1], dims_in[2] // 2, 2)
    first_part = pair_view[..., 0]
    second_part = pair_view[..., 1]
    cosine = cosine[:, None, :]
    sine_part = sine_part[:, None, :]
    turned = jnp.stack([cosine * first_part - sine_part * second_part, sine_part * first_part + cosine * second_part], axis=-1)
    return turned.reshape(dims_in)

def rms_gain(tensor, gain_vec):
    return tensor * lax.rsqrt(lax.optimization_barrier(jnp.mean(tensor * tensor, axis=-1, keepdims=True)) + 1e-06) * gain_vec

def modulate(features, shift_vec, scale_vec):
    row_mean = lax.optimization_barrier(jnp.mean(features, axis=-1, keepdims=True))
    row_var = lax.optimization_barrier(jnp.mean(features * features, axis=-1, keepdims=True)) - row_mean * row_mean
    return (features - row_mean) * lax.rsqrt(row_var + 1e-06) * (1.0 + scale_vec) + shift_vec

def sigma_at(step_now):
    time_now = 1.0 - step_now.astype(jnp.float32) / STEPS
    return SHIFT * time_now / (1.0 + (SHIFT - 1.0) * time_now)

def key_live(text_count):
    offset = jnp.arange(L, dtype=jnp.int32) % ROWS_DEV
    block_pos = jnp.arange(L, dtype=jnp.int32) // ROWS_DEV
    text_index = block_pos * TXT_DEV + offset - IMG_DEV
    return (offset < IMG_DEV) | (text_index < text_count)

def one_sequence(hidden_seq, ids_seq, layer_terms, final_terms, text_count, qkv_weight, q_gain, k_gain, out_weight, final_weight):
    features = hidden_seq.astype(jnp.float32)
    modulated = modulate(features, layer_terms[0], layer_terms[1]).astype(jnp.bfloat16)
    head_cols = HEADS * HEAD_DIM
    projected = jnp.dot(modulated, qkv_weight.reshape(D, 3 * head_cols), preferred_element_type=jnp.float32)
    projected = projected.reshape(L, 3, HEADS, HEAD_DIM)
    cosine, sine_part = rope_angles(ids_seq)
    queries = rotate(rms_gain(projected[:, 0], q_gain), cosine, sine_part).astype(jnp.bfloat16)
    key_rot = rotate(rms_gain(projected[:, 1], k_gain), cosine, sine_part).astype(jnp.bfloat16)
    values = projected[:, 2].astype(jnp.bfloat16)
    is_live = key_live(text_count)

    def one_head(head_parts):
        head_q, head_k, head_v = head_parts
        scores = jnp.dot(head_q, head_k.T, preferred_element_type=jnp.float32) * HEAD_DIM ** (-0.5)
        scores = jnp.where(is_live[None, :], scores, -jnp.inf)
        row_max = lax.optimization_barrier(jnp.max(scores, axis=1, keepdims=True))
        exps = jnp.exp(scores - row_max)
        row_sum = lax.optimization_barrier(jnp.sum(exps, axis=1, keepdims=True))
        attended = jnp.dot(exps.astype(jnp.bfloat16), head_v, preferred_element_type=jnp.float32) / row_sum
        return (attended.astype(jnp.bfloat16), (row_max + jnp.log(row_sum))[:, 0])
    heads_out, log_sums = lax.map(one_head, (queries.transpose(1, 0, 2), key_rot.transpose(1, 0, 2), values.transpose(1, 0, 2)))
    attn_flat = heads_out.transpose(1, 0, 2).reshape(L, head_cols)
    update = jnp.dot(attn_flat, out_weight, preferred_element_type=jnp.float32)
    new_seq = (features + layer_terms[2] * update).astype(jnp.bfloat16)
    image_rows = new_seq.reshape(S, ROWS_DEV, D)[:, :IMG_DEV].reshape(IMG, D).astype(jnp.float32)
    final_in = modulate(image_rows, final_terms[0], final_terms[1])
    velocity = jnp.dot(final_in, final_weight.astype(jnp.float32), precision=lax.Precision.HIGHEST)
    return (new_seq, log_sums, velocity)

def reference(hidden, positions, lengths, step_index, layer_mod, final_mod, qkv_weight, q_gain, k_gain, out_weight, final_weight, latents):
    hidden_list = []
    lse_list = []
    velocity_list = []
    for seq_pos in range(SEQS):
        new_seq, log_sums, velocity = one_sequence(hidden[seq_pos * L:(seq_pos + 1) * L], positions[:, seq_pos * L:(seq_pos + 1) * L], layer_mod[seq_pos], final_mod[seq_pos], lengths[seq_pos], qkv_weight, q_gain, k_gain, out_weight, final_weight)
        hidden_list.append(new_seq)
        lse_list.append(log_sums)
        velocity_list.append(velocity)
    step_now = step_index[0]
    time_step = sigma_at(step_now + 1) - sigma_at(step_now)
    results = []
    for prompt in range(PROMPTS):
        cond_vel = velocity_list[2 * prompt]
        uncond_vel = velocity_list[2 * prompt + 1]
        guided = uncond_vel + GUIDE * (cond_vel - uncond_vel)
        ordered = guided.reshape(S, 2, HALF, CH).transpose(1, 0, 2, 3).reshape(IMG, CH)
        results.append(latents[prompt * IMG:(prompt + 1) * IMG] + time_step * ordered)
    return (jnp.concatenate(hidden_list, axis=0), jnp.concatenate(lse_list, axis=1), jnp.concatenate(results, axis=0))
```

```python
import jax
import jax.numpy as jnp
from jax import lax
from jax.sharding import PartitionSpec as P

ROPE_T = 16
ROPE_H = 56
ROPE_W = 56
STEPS = 8
IMG_DEV = 512
TXT_DEV = 64


GUIDE = 3.5
SHIFT = 3.0


def swapped(block, axis, bit):
    count = lax.axis_size(axis)
    route = []
    for low in range(count):
        high = low | 1 << bit
        if high != low and high < count:
            route += [(low, high), (high, low)]
    return lax.ppermute(block, axis, route)


def seq_route(spread, move):
    count_x = spread // 2
    route = []
    for group in range(4):
        for shard in range(spread):
            dest_x, dest_z = move(shard // 2, shard % 2, count_x)
            route.append((group * spread + shard, group * spread + (dest_x % count_x) * 2 + dest_z))
    return route


def rope_tables(ids_block):
    angle_parts = []
    for axis_pos, rope_width in ((0, ROPE_T), (1, ROPE_H), (2, ROPE_W)):
        frequencies = 10000.0 ** (-jnp.arange(0, rope_width, 2).astype(jnp.float32) / rope_width)
        angle_parts.append(ids_block[axis_pos].astype(jnp.float32)[:, None] * frequencies[None, :])
    angles = jnp.concatenate(angle_parts, axis=1)
    angles = jnp.repeat(angles, 2, axis=1)
    even = (jnp.arange(angles.shape[1]) % 2 == 0)[None, :]
    sine = jnp.sin(angles)
    return (jnp.cos(angles), jnp.where(even, -sine, sine), even)


def rotate(tensor, cosine, signed_sine, even):
    partner = jnp.where(
        even[None], jnp.roll(tensor, -1, axis=-1), jnp.roll(tensor, 1, axis=-1)
    )
    return tensor * cosine[None] + partner * signed_sine[None]


def rms_gain(tensor, gain_vec):
    return tensor * lax.rsqrt(jnp.mean(tensor * tensor, axis=-1, keepdims=True) + 1e-06) * gain_vec


def modulate(features, shift_vec, scale_vec):
    row_mean = jnp.mean(features, axis=-1, keepdims=True)
    row_var = jnp.mean(features * features, axis=-1, keepdims=True) - row_mean * row_mean
    return (features - row_mean) * lax.rsqrt(row_var + 1e-06) * (1.0 + scale_vec) + shift_vec


def sigma_at(step_now):
    time_now = 1.0 - step_now.astype(jnp.float32) / STEPS
    return SHIFT * time_now / (1.0 + (SHIFT - 1.0) * time_now)


def fold_block(state, queries, key_block, value_block, shard, text_count):
    row_max, row_sum, weighted = state
    rows_dev = key_block.shape[1]
    offset = jnp.arange(rows_dev, dtype=jnp.int32)
    text_index = shard * TXT_DEV + offset - IMG_DEV
    is_live = (offset < IMG_DEV) | (text_index < text_count)
    score_scale = queries.shape[-1] ** (-0.5)
    scores = (
        jnp.einsum("hqd,hkd->hqk", queries, key_block, preferred_element_type=jnp.float32)
        * score_scale
    )
    scores = jnp.where(is_live[None, None, :], scores, -jnp.inf)
    new_max = jnp.maximum(row_max, jnp.max(scores, axis=2))
    exps = jnp.exp(scores - new_max[:, :, None])
    decay = jnp.exp(row_max - new_max)
    row_sum = row_sum * decay + jnp.sum(exps, axis=2)
    weighted = weighted * decay[:, :, None] + jnp.einsum(
        "hqk,hkd->hqd", exps.astype(jnp.bfloat16), value_block, preferred_element_type=jnp.float32
    )
    return (new_max, row_sum, weighted)


def tp_sum(tree):
    count = lax.axis_size("tp")
    bit = 0
    while 1 << bit < count:
        far = swapped(tree, "tp", bit)
        tree = jax.tree.map(lambda a, b: a + b, tree, far)
        bit += 1
    return tree


def on_device(
    hidden,
    positions,
    lengths,
    step_index,
    layer_mod,
    final_mod,
    qkv_weight,
    q_gain,
    k_gain,
    out_weight,
    final_weight,
    latents,
):
    spread = lax.axis_size("seq") // 4
    bit_count = spread.bit_length() - 1
    seq_pos = lax.axis_index("seq")
    local_seq = seq_pos // spread
    shard_pos = seq_pos % spread
    count_x = spread // 2
    my_x = shard_pos // 2
    my_z = shard_pos % 2
    tp_pos = lax.axis_index("tp")
    local_width = hidden.shape[1]
    gathered = lax.all_gather(hidden, "tp", axis=1, tiled=True)
    model_width = gathered.shape[1]
    rows_dev = gathered.shape[0]
    layer_terms = lax.dynamic_index_in_dim(layer_mod, local_seq, 0, keepdims=False)
    text_count = lax.dynamic_index_in_dim(lengths, local_seq, 0, keepdims=False)
    modulated = modulate(gathered.astype(jnp.float32), layer_terms[0], layer_terms[1]).astype(
        jnp.bfloat16
    )
    head_dim = q_gain.shape[0]
    head_cols = qkv_weight.shape[2]
    heads_here = head_cols // head_dim
    weight4 = qkv_weight.reshape(model_width, 3, heads_here, head_dim)
    projected = jnp.einsum(
        "rf,fchd->chrd", modulated, weight4, preferred_element_type=jnp.float32
    )
    cosine, signed_sine, even = rope_tables(positions)
    queries = rotate(rms_gain(projected[0], q_gain), cosine, signed_sine, even).astype(jnp.bfloat16)
    key_rot = rotate(rms_gain(projected[1], k_gain), cosine, signed_sine, even).astype(jnp.bfloat16)
    values = projected[2].astype(jnp.bfloat16)
    own = jnp.stack([key_rot, values])

    to_left = seq_route(spread, lambda x, z, n: (x - 1, z))
    to_right = seq_route(spread, lambda x, z, n: (x + 1, z))
    to_other_z = seq_route(spread, lambda x, z, n: (x, 1 - z))

    def shard_of(x, z):
        return (x % count_x) * 2 + z

    got_z = lax.ppermute(own, "seq", to_other_z)
    got_right = lax.ppermute(own, "seq", to_left)
    got_left = lax.ppermute(own, "seq", to_right)

    softmax_state = (
        jnp.full((heads_here, rows_dev), -jnp.inf, jnp.float32),
        jnp.zeros((heads_here, rows_dev), jnp.float32),
        jnp.zeros((heads_here, rows_dev, head_dim), jnp.float32),
    )
    softmax_state = fold_block(softmax_state, queries, own[0], own[1], shard_pos, text_count)

    z_from_right = lax.ppermute(got_z, "seq", to_left)
    z_from_left = lax.ppermute(got_z, "seq", to_right)
    far_keys = lax.ppermute(got_right[0], "seq", to_left)
    far_values = lax.ppermute(got_left[1], "seq", to_right)

    other_z = 1 - my_z
    softmax_state = fold_block(
        softmax_state, queries, got_z[0], got_z[1], shard_of(my_x, other_z), text_count
    )
    softmax_state = fold_block(
        softmax_state, queries, got_right[0], got_right[1], shard_of(my_x + 1, my_z), text_count
    )
    softmax_state = fold_block(
        softmax_state, queries, got_left[0], got_left[1], shard_of(my_x - 1, my_z), text_count
    )

    far_z_keys = lax.ppermute(z_from_right[0], "seq", to_left)
    far_z_values = lax.ppermute(z_from_left[1], "seq", to_right)

    softmax_state = fold_block(
        softmax_state, queries, z_from_right[0], z_from_right[1], shard_of(my_x + 1, other_z), text_count
    )
    softmax_state = fold_block(
        softmax_state, queries, z_from_left[0], z_from_left[1], shard_of(my_x - 1, other_z), text_count
    )
    softmax_state = fold_block(
        softmax_state, queries, far_keys, far_values, shard_of(my_x + 2, my_z), text_count
    )
    softmax_state = fold_block(
        softmax_state, queries, far_z_keys, far_z_values, shard_of(my_x + 2, other_z), text_count
    )

    row_max, row_sum, weighted = softmax_state
    attended = (weighted / row_sum[:, :, None]).astype(jnp.bfloat16)
    log_sums = row_max + jnp.log(row_sum)
    out_weight3 = out_weight.reshape(heads_here, head_dim, out_weight.shape[1])
    partial_out = jnp.einsum(
        "hrd,hdf->rf", attended, out_weight3, preferred_element_type=jnp.float32
    )
    update = lax.psum_scatter(
        partial_out.astype(jnp.bfloat16), "tp", scatter_dimension=1, tiled=True
    ).astype(jnp.float32)
    gate_slice = lax.dynamic_slice_in_dim(layer_terms[2], tp_pos * local_width, local_width, 0)
    new_hidden = (hidden.astype(jnp.float32) + gate_slice * update).astype(jnp.bfloat16)

    final_terms = lax.dynamic_index_in_dim(final_mod, local_seq, 0, keepdims=False)
    final_shift = lax.dynamic_slice_in_dim(final_terms[0], tp_pos * local_width, local_width, 0)
    final_scale = lax.dynamic_slice_in_dim(final_terms[1], tp_pos * local_width, local_width, 0)
    image_rows = new_hidden[:IMG_DEV].astype(jnp.float32)
    weight = final_weight.astype(jnp.float32)
    scale_one = 1.0 + final_scale
    highest = lax.Precision.HIGHEST
    terms = (
        jnp.sum(image_rows, axis=1),
        jnp.sum(image_rows * image_rows, axis=1),
        jnp.dot(image_rows * scale_one, weight, precision=highest),
        jnp.dot(scale_one[None, :], weight, precision=highest),
        jnp.dot(final_shift[None, :], weight, precision=highest),
    )
    row_sums, squares, scaled_proj, scale_proj, shift_proj = tp_sum(terms)
    row_mean = row_sums / model_width
    inv_std = lax.rsqrt(squares / model_width - row_mean * row_mean + 1e-06)
    velocity = (
        inv_std[:, None] * (scaled_proj - row_mean[:, None] * scale_proj) + shift_proj
    )

    half_rows = IMG_DEV // 2
    is_cond = local_seq % 2 == 0
    outgoing = jnp.where(is_cond, velocity[half_rows:], velocity[:half_rows])
    partner_half = swapped(outgoing, "seq", bit_count)
    own_half = jnp.where(is_cond, velocity[:half_rows], velocity[half_rows:])
    cond_vel = jnp.where(is_cond, own_half, partner_half)
    uncond_vel = jnp.where(is_cond, partner_half, own_half)
    guided = uncond_vel + GUIDE * (cond_vel - uncond_vel)
    step_now = step_index[0]
    time_step = sigma_at(step_now + 1) - sigma_at(step_now)
    return (new_hidden, log_sums, latents + time_step * guided)


def solution(mesh):
    return jax.shard_map(
        on_device,
        mesh=mesh,
        in_specs=(
            P(("pair", "seq"), "tp"),
            P(None, ("pair", "seq")),
            P("pair"),
            P(),
            P("pair", None, None),
            P("pair", None, None),
            P(None, None, "tp"),
            P(),
            P(),
            P("tp", None),
            P("tp", None),
            P(("pair", "seq"), None),
        ),
        out_specs=(P(("pair", "seq"), "tp"), P("tp", ("pair", "seq")), P(("pair", "seq"), None)),
        check_vma=False,
    )
```

```python
import jax
import jax.numpy as jnp
from jax import lax
from jax.sharding import PartitionSpec as P

ROPE_T = 16
ROPE_H = 56
ROPE_W = 56
STEPS = 8
IMG_DEV = 512
TXT_DEV = 64


GUIDE = 3.5
SHIFT = 3.0


def swapped(block, axis, bit):
    count = lax.axis_size(axis)
    route = []
    for low in range(count):
        high = low | 1 << bit
        if high != low and high < count:
            route += [(low, high), (high, low)]
    return lax.ppermute(block, axis, route)


def seq_route(spread, move):
    count_x = spread // 2
    route = []
    for group in range(4):
        for shard in range(spread):
            dest_x, dest_z = move(shard // 2, shard % 2, count_x)
            route.append((group * spread + shard, group * spread + (dest_x % count_x) * 2 + dest_z))
    return route


def rope_tables(ids_block):
    angle_parts = []
    for axis_pos, rope_width in ((0, ROPE_T), (1, ROPE_H), (2, ROPE_W)):
        frequencies = 10000.0 ** (-jnp.arange(0, rope_width, 2).astype(jnp.float32) / rope_width)
        angle_parts.append(ids_block[axis_pos].astype(jnp.float32)[:, None] * frequencies[None, :])
    angles = jnp.concatenate(angle_parts, axis=1)
    angles = jnp.repeat(angles, 2, axis=1)
    even = (jnp.arange(angles.shape[1]) % 2 == 0)[None, :]
    sine = jnp.sin(angles)
    return (jnp.cos(angles), jnp.where(even, -sine, sine), even)


def rotate(tensor, cosine, signed_sine, even):
    partner = jnp.where(
        even[None], jnp.roll(tensor, -1, axis=-1), jnp.roll(tensor, 1, axis=-1)
    )
    return tensor * cosine[None] + partner * signed_sine[None]


def rms_gain(tensor, gain_vec):
    return tensor * lax.rsqrt(jnp.mean(tensor * tensor, axis=-1, keepdims=True) + 1e-06) * gain_vec


def modulate(features, shift_vec, scale_vec):
    row_mean = jnp.mean(features, axis=-1, keepdims=True)
    row_var = jnp.mean(features * features, axis=-1, keepdims=True) - row_mean * row_mean
    return (features - row_mean) * lax.rsqrt(row_var + 1e-06) * (1.0 + scale_vec) + shift_vec


def sigma_at(step_now):
    time_now = 1.0 - step_now.astype(jnp.float32) / STEPS
    return SHIFT * time_now / (1.0 + (SHIFT - 1.0) * time_now)


def live_keys(rows, offset_base, shard, text_count):
    offset = offset_base + jnp.arange(rows, dtype=jnp.int32)
    text_index = shard * TXT_DEV + offset - IMG_DEV
    return (offset < IMG_DEV) | (text_index < text_count)


def fold_keys(state, queries, key_block, value_block, is_live):
    row_max, row_sum, weighted = state
    score_scale = queries.shape[-1] ** (-0.5)
    scores = (
        jnp.einsum("hqd,hkd->hqk", queries, key_block, preferred_element_type=jnp.float32)
        * score_scale
    )
    scores = jnp.where(is_live[None, None, :], scores, -jnp.inf)
    new_max = jnp.maximum(row_max, jnp.max(scores, axis=2))
    exps = jnp.exp(scores - new_max[:, :, None])
    decay = jnp.exp(row_max - new_max)
    row_sum = row_sum * decay + jnp.sum(exps, axis=2)
    weighted = weighted * decay[:, :, None] + jnp.einsum(
        "hqk,hkd->hqd", exps.astype(jnp.bfloat16), value_block, preferred_element_type=jnp.float32
    )
    return (new_max, row_sum, weighted)


def fold_block(state, queries, key_block, value_block, shard, offset_base, text_count):
    is_live = live_keys(key_block.shape[1], offset_base, shard, text_count)
    return fold_keys(state, queries, key_block, value_block, is_live)


def fold_many(state, queries, key_blocks, value_blocks, shards, offset_base, text_count):
    rows = key_blocks.shape[1] // len(shards)
    is_live = jnp.concatenate(
        [live_keys(rows, offset_base, shard, text_count) for shard in shards]
    )
    return fold_keys(state, queries, key_blocks, value_blocks, is_live)


def tp_sum(tree):
    count = lax.axis_size("tp")
    bit = 0
    while 1 << bit < count:
        far = swapped(tree, "tp", bit)
        tree = jax.tree.map(lambda a, b: a + b, tree, far)
        bit += 1
    return tree


def exchange(own, shard_pos, spread):
    count_x = spread // 2
    my_x = shard_pos // 2
    my_z = shard_pos % 2
    other_z = 1 - my_z
    to_left = seq_route(spread, lambda x, z, n: (x - 1, z))
    to_right = seq_route(spread, lambda x, z, n: (x + 1, z))
    to_other_z = seq_route(spread, lambda x, z, n: (x, 1 - z))

    def shard_of(x, z):
        return (x % count_x) * 2 + z

    got_z = lax.ppermute(own, "seq", to_other_z)
    got_right = lax.ppermute(own, "seq", to_left)
    got_left = lax.ppermute(own, "seq", to_right)
    z_from_right, far_keys = lax.ppermute((got_z, got_right[0]), "seq", to_left)
    z_from_left, far_values = lax.ppermute((got_z, got_left[1]), "seq", to_right)
    far_z_keys = lax.ppermute(z_from_right[0], "seq", to_left)
    far_z_values = lax.ppermute(z_from_left[1], "seq", to_right)
    return [
        (own[0], own[1], shard_pos),
        (got_z[0], got_z[1], shard_of(my_x, other_z)),
        (got_right[0], got_right[1], shard_of(my_x + 1, my_z)),
        (got_left[0], got_left[1], shard_of(my_x - 1, my_z)),
        (z_from_right[0], z_from_right[1], shard_of(my_x + 1, other_z)),
        (z_from_left[0], z_from_left[1], shard_of(my_x - 1, other_z)),
        (far_keys, far_values, shard_of(my_x + 2, my_z)),
        (far_z_keys, far_z_values, shard_of(my_x + 2, other_z)),
    ]


def on_device(
    hidden,
    positions,
    lengths,
    step_index,
    layer_mod,
    final_mod,
    qkv_weight,
    q_gain,
    k_gain,
    out_weight,
    final_weight,
    latents,
):
    spread = lax.axis_size("seq") // 4
    assert spread // 2 == 4
    bit_count = spread.bit_length() - 1
    seq_pos = lax.axis_index("seq")
    local_seq = seq_pos // spread
    shard_pos = seq_pos % spread
    tp_pos = lax.axis_index("tp")
    local_width = hidden.shape[1]
    rows_dev = hidden.shape[0]
    split = rows_dev // 2
    model_width = local_width * lax.axis_size("tp")
    layer_terms = lax.dynamic_index_in_dim(layer_mod, local_seq, 0, keepdims=False)
    text_count = lax.dynamic_index_in_dim(lengths, local_seq, 0, keepdims=False)
    head_dim = q_gain.shape[0]
    head_cols = qkv_weight.shape[2]
    heads_here = head_cols // head_dim
    weight4 = qkv_weight.reshape(model_width, 3, heads_here, head_dim)
    cosine, signed_sine, even = rope_tables(positions)

    def gather(row_lo, row_hi):
        return lax.all_gather(hidden[row_lo:row_hi], "tp", axis=1, tiled=True)

    def project(gathered, row_lo, row_hi):
        modulated = modulate(
            gathered.astype(jnp.float32), layer_terms[0], layer_terms[1]
        ).astype(jnp.bfloat16)
        projected = jnp.einsum(
            "rf,fchd->chrd", modulated, weight4, preferred_element_type=jnp.float32
        )
        cos_part = cosine[row_lo:row_hi]
        sin_part = signed_sine[row_lo:row_hi]
        queries = rotate(rms_gain(projected[0], q_gain), cos_part, sin_part, even).astype(
            jnp.bfloat16
        )
        key_rot = rotate(rms_gain(projected[1], k_gain), cos_part, sin_part, even).astype(
            jnp.bfloat16
        )
        values = projected[2].astype(jnp.bfloat16)
        return queries, jnp.stack([key_rot, values])

    gathered_a = gather(0, split)
    queries_a, own_a = project(gathered_a, 0, split)
    blocks_a = exchange(own_a, shard_pos, spread)
    hold = blocks_a[1][0][0, 0, 0] * 0
    hidden_b = hidden[split:] + hold
    gathered_b = lax.all_gather(hidden_b, "tp", axis=1, tiled=True)
    queries_b, own_b = project(gathered_b, split, rows_dev)
    blocks_b = exchange(own_b, shard_pos, spread)

    def empty_state(rows):
        return (
            jnp.full((heads_here, rows), -jnp.inf, jnp.float32),
            jnp.zeros((heads_here, rows), jnp.float32),
            jnp.zeros((heads_here, rows, head_dim), jnp.float32),
        )

    state_a = empty_state(split)
    for key_block, value_block, shard in blocks_a:
        state_a = fold_block(state_a, queries_a, key_block, value_block, shard, 0, text_count)
    state_b = empty_state(rows_dev - split)
    all_keys = jnp.concatenate([blk[0] for blk in blocks_a], axis=1)
    all_values = jnp.concatenate([blk[1] for blk in blocks_a], axis=1)
    state_b = fold_many(
        state_b, queries_b, all_keys, all_values, [blk[2] for blk in blocks_a], 0, text_count
    )
    queries = jnp.concatenate([queries_a, queries_b], axis=1)
    softmax_state = jax.tree.map(lambda a, b: jnp.concatenate([a, b], axis=1), state_a, state_b)
    for key_block, value_block, shard in blocks_b:
        softmax_state = fold_block(
            softmax_state, queries, key_block, value_block, shard, split, text_count
        )

    row_max, row_sum, weighted = softmax_state
    attended = (weighted / row_sum[:, :, None]).astype(jnp.bfloat16)
    log_sums = row_max + jnp.log(row_sum)
    out_weight3 = out_weight.reshape(heads_here, head_dim, out_weight.shape[1])
    partial_out = jnp.einsum(
        "hrd,hdf->rf", attended, out_weight3, preferred_element_type=jnp.float32
    )
    update = lax.psum_scatter(
        partial_out.astype(jnp.bfloat16), "tp", scatter_dimension=1, tiled=True
    ).astype(jnp.float32)
    gate_slice = lax.dynamic_slice_in_dim(layer_terms[2], tp_pos * local_width, local_width, 0)
    new_hidden = (hidden.astype(jnp.float32) + gate_slice * update).astype(jnp.bfloat16)

    final_terms = lax.dynamic_index_in_dim(final_mod, local_seq, 0, keepdims=False)
    final_shift = lax.dynamic_slice_in_dim(final_terms[0], tp_pos * local_width, local_width, 0)
    final_scale = lax.dynamic_slice_in_dim(final_terms[1], tp_pos * local_width, local_width, 0)
    image_rows = new_hidden[:IMG_DEV].astype(jnp.float32)
    weight = final_weight.astype(jnp.float32)
    scale_one = 1.0 + final_scale
    highest = lax.Precision.HIGHEST
    terms = (
        jnp.sum(image_rows, axis=1),
        jnp.sum(image_rows * image_rows, axis=1),
        jnp.dot(image_rows * scale_one, weight, precision=highest),
        jnp.dot(scale_one[None, :], weight, precision=highest),
        jnp.dot(final_shift[None, :], weight, precision=highest),
    )
    row_sums, squares, scaled_proj, scale_proj, shift_proj = tp_sum(terms)
    row_mean = row_sums / model_width
    inv_std = lax.rsqrt(squares / model_width - row_mean * row_mean + 1e-06)
    velocity = (
        inv_std[:, None] * (scaled_proj - row_mean[:, None] * scale_proj) + shift_proj
    )

    half_rows = IMG_DEV // 2
    is_cond = local_seq % 2 == 0
    outgoing = jnp.where(is_cond, velocity[half_rows:], velocity[:half_rows])
    partner_half = swapped(outgoing, "seq", bit_count)
    own_half = jnp.where(is_cond, velocity[:half_rows], velocity[half_rows:])
    cond_vel = jnp.where(is_cond, own_half, partner_half)
    uncond_vel = jnp.where(is_cond, partner_half, own_half)
    guided = uncond_vel + GUIDE * (cond_vel - uncond_vel)
    step_now = step_index[0]
    time_step = sigma_at(step_now + 1) - sigma_at(step_now)
    return (new_hidden, log_sums, latents + time_step * guided)


def solution(mesh):
    return jax.shard_map(
        on_device,
        mesh=mesh,
        in_specs=(
            P(("pair", "seq"), "tp"),
            P(None, ("pair", "seq")),
            P("pair"),
            P(),
            P("pair", None, None),
            P("pair", None, None),
            P(None, None, "tp"),
            P(),
            P(),
            P("tp", None),
            P("tp", None),
            P(("pair", "seq"), None),
        ),
        out_specs=(P(("pair", "seq"), "tp"), P("tp", ("pair", "seq")), P(("pair", "seq"), None)),
        check_vma=False,
    )
```

```python
import jax
import jax.numpy as jnp
from jax import lax
from jax.sharding import PartitionSpec as P

ROPE_T = 16
ROPE_H = 56
ROPE_W = 56
STEPS = 8
IMG_DEV = 512
TXT_DEV = 64


GUIDE = 3.5
SHIFT = 3.0


def swapped(block, axis, bit):
    count = lax.axis_size(axis)
    route = []
    for low in range(count):
        high = low | 1 << bit
        if high != low and high < count:
            route += [(low, high), (high, low)]
    return lax.ppermute(block, axis, route)


def seq_route(spread, move):
    count_x = spread // 2
    route = []
    for group in range(4):
        for shard in range(spread):
            dest_x, dest_z = move(shard // 2, shard % 2, count_x)
            route.append((group * spread + shard, group * spread + (dest_x % count_x) * 2 + dest_z))
    return route


def rope_tables(ids_block):
    angle_parts = []
    for axis_pos, rope_width in ((0, ROPE_T), (1, ROPE_H), (2, ROPE_W)):
        frequencies = 10000.0 ** (-jnp.arange(0, rope_width, 2).astype(jnp.float32) / rope_width)
        angle_parts.append(ids_block[axis_pos].astype(jnp.float32)[:, None] * frequencies[None, :])
    angles = jnp.concatenate(angle_parts, axis=1)
    angles = jnp.repeat(angles, 2, axis=1)
    even = (jnp.arange(angles.shape[1]) % 2 == 0)[None, :]
    sine = jnp.sin(angles)
    return (jnp.cos(angles), jnp.where(even, -sine, sine), even)


def rotate(tensor, cosine, signed_sine, even):
    partner = jnp.where(
        even[None], jnp.roll(tensor, -1, axis=-1), jnp.roll(tensor, 1, axis=-1)
    )
    return tensor * cosine[None] + partner * signed_sine[None]


def rms_gain(tensor, gain_vec):
    return tensor * lax.rsqrt(jnp.mean(tensor * tensor, axis=-1, keepdims=True) + 1e-06) * gain_vec


def modulate(features, shift_vec, scale_vec):
    row_mean = jnp.mean(features, axis=-1, keepdims=True)
    row_var = jnp.mean(features * features, axis=-1, keepdims=True) - row_mean * row_mean
    return (features - row_mean) * lax.rsqrt(row_var + 1e-06) * (1.0 + scale_vec) + shift_vec


def sigma_at(step_now):
    time_now = 1.0 - step_now.astype(jnp.float32) / STEPS
    return SHIFT * time_now / (1.0 + (SHIFT - 1.0) * time_now)


def fold_block(state, queries, key_block, value_block, shard, text_count):
    row_max, row_sum, weighted = state
    rows_dev = key_block.shape[1]
    offset = jnp.arange(rows_dev, dtype=jnp.int32)
    text_index = shard * TXT_DEV + offset - IMG_DEV
    is_live = (offset < IMG_DEV) | (text_index < text_count)
    score_scale = queries.shape[-1] ** (-0.5)
    scores = (
        jnp.einsum("hqd,hkd->hqk", queries, key_block, preferred_element_type=jnp.float32)
        * score_scale
    )
    scores = jnp.where(is_live[None, None, :], scores, -jnp.inf)
    new_max = jnp.maximum(row_max, jnp.max(scores, axis=2))
    exps = jnp.exp(scores - new_max[:, :, None])
    decay = jnp.exp(row_max - new_max)
    row_sum = row_sum * decay + jnp.sum(exps, axis=2)
    weighted = weighted * decay[:, :, None] + jnp.einsum(
        "hqk,hkd->hqd", exps.astype(jnp.bfloat16), value_block, preferred_element_type=jnp.float32
    )
    return (new_max, row_sum, weighted)


def tp_sum(tree):
    count = lax.axis_size("tp")
    bit = 0
    while 1 << bit < count:
        far = swapped(tree, "tp", bit)
        tree = jax.tree.map(lambda a, b: a + b, tree, far)
        bit += 1
    return tree


def on_device(
    hidden,
    positions,
    lengths,
    step_index,
    layer_mod,
    final_mod,
    qkv_weight,
    q_gain,
    k_gain,
    out_weight,
    final_weight,
    latents,
):
    spread = lax.axis_size("seq") // 4
    bit_count = spread.bit_length() - 1
    seq_pos = lax.axis_index("seq")
    local_seq = seq_pos // spread
    shard_pos = seq_pos % spread
    count_x = spread // 2
    my_x = shard_pos // 2
    my_z = shard_pos % 2
    tp_pos = lax.axis_index("tp")
    local_width = hidden.shape[1]
    gathered = lax.all_gather(hidden, "tp", axis=1, tiled=True)
    model_width = gathered.shape[1]
    rows_dev = gathered.shape[0]
    layer_terms = lax.dynamic_index_in_dim(layer_mod, local_seq, 0, keepdims=False)
    text_count = lax.dynamic_index_in_dim(lengths, local_seq, 0, keepdims=False)
    modulated = modulate(gathered.astype(jnp.float32), layer_terms[0], layer_terms[1]).astype(
        jnp.bfloat16
    )
    head_dim = q_gain.shape[0]
    head_cols = qkv_weight.shape[2]
    heads_here = head_cols // head_dim
    weight4 = qkv_weight.reshape(model_width, 3, heads_here, head_dim)
    projected = jnp.einsum(
        "rf,fchd->chrd", modulated, weight4, preferred_element_type=jnp.float32
    )
    cosine, signed_sine, even = rope_tables(positions)
    queries = rotate(rms_gain(projected[0], q_gain), cosine, signed_sine, even).astype(jnp.bfloat16)
    key_rot = rotate(rms_gain(projected[1], k_gain), cosine, signed_sine, even).astype(jnp.bfloat16)
    values = projected[2].astype(jnp.bfloat16)
    own = jnp.stack([key_rot, values])

    to_left = seq_route(spread, lambda x, z, n: (x - 1, z))
    to_right = seq_route(spread, lambda x, z, n: (x + 1, z))
    to_other_z = seq_route(spread, lambda x, z, n: (x, 1 - z))

    def shard_of(x, z):
        return (x % count_x) * 2 + z

    got_z = lax.ppermute(own, "seq", to_other_z)
    got_right = lax.ppermute(own, "seq", to_left)
    got_left = lax.ppermute(own, "seq", to_right)

    softmax_state = (
        jnp.full((heads_here, rows_dev), -jnp.inf, jnp.float32),
        jnp.zeros((heads_here, rows_dev), jnp.float32),
        jnp.zeros((heads_here, rows_dev, head_dim), jnp.float32),
    )
    softmax_state = fold_block(softmax_state, queries, own[0], own[1], shard_pos, text_count)

    z_from_right = lax.ppermute(got_z, "seq", to_left)
    z_from_left = lax.ppermute(got_z, "seq", to_right)
    far_keys = lax.ppermute(got_right[0], "seq", to_left)
    far_values = lax.ppermute(got_left[1], "seq", to_right)

    other_z = 1 - my_z
    softmax_state = fold_block(
        softmax_state, queries, got_z[0], got_z[1], shard_of(my_x, other_z), text_count
    )
    softmax_state = fold_block(
        softmax_state, queries, got_right[0], got_right[1], shard_of(my_x + 1, my_z), text_count
    )
    softmax_state = fold_block(
        softmax_state, queries, got_left[0], got_left[1], shard_of(my_x - 1, my_z), text_count
    )

    far_z_keys = lax.ppermute(z_from_right[0], "seq", to_left)
    far_z_values = lax.ppermute(z_from_left[1], "seq", to_right)

    softmax_state = fold_block(
        softmax_state, queries, z_from_right[0], z_from_right[1], shard_of(my_x + 1, other_z), text_count
    )
    softmax_state = fold_block(
        softmax_state, queries, z_from_left[0], z_from_left[1], shard_of(my_x - 1, other_z), text_count
    )
    softmax_state = fold_block(
        softmax_state, queries, far_keys, far_values, shard_of(my_x + 2, my_z), text_count
    )
    softmax_state = fold_block(
        softmax_state, queries, far_z_keys, far_z_values, shard_of(my_x + 2, other_z), text_count
    )

    row_max, row_sum, weighted = softmax_state
    attended = (weighted / row_sum[:, :, None]).astype(jnp.bfloat16)
    log_sums = row_max + jnp.log(row_sum)
    tp_count = lax.axis_size("tp")
    hold = jnp.minimum(jnp.abs(queries[0, 0, 0]), 0).astype(out_weight.dtype)
    attended_parts = [attended]
    weight_parts = [lax.dynamic_slice_in_dim(out_weight, tp_pos * local_width, local_width, 1)]
    for shift in range(1, tp_count):
        route = [(src, (src + shift) % tp_count) for src in range(tp_count)]
        dest = (tp_pos + shift) % tp_count
        weight_send = lax.dynamic_slice_in_dim(out_weight, dest * local_width, local_width, 1)
        weight_parts.append(lax.ppermute(weight_send + hold, "tp", route))
        attended_parts.append(lax.ppermute(attended, "tp", route))
    all_attended = jnp.stack(attended_parts)
    all_weights = jnp.stack(weight_parts).reshape(tp_count, heads_here, head_dim, local_width)
    update = jnp.einsum(
        "khrd,khdf->rf", all_attended, all_weights, preferred_element_type=jnp.float32
    )
    gate_slice = lax.dynamic_slice_in_dim(layer_terms[2], tp_pos * local_width, local_width, 0)
    new_hidden = (hidden.astype(jnp.float32) + gate_slice * update).astype(jnp.bfloat16)

    final_terms = lax.dynamic_index_in_dim(final_mod, local_seq, 0, keepdims=False)
    final_shift = lax.dynamic_slice_in_dim(final_terms[0], tp_pos * local_width, local_width, 0)
    final_scale = lax.dynamic_slice_in_dim(final_terms[1], tp_pos * local_width, local_width, 0)
    image_rows = new_hidden[:IMG_DEV].astype(jnp.float32)
    weight = final_weight.astype(jnp.float32)
    scale_one = 1.0 + final_scale
    highest = lax.Precision.HIGHEST
    terms = (
        jnp.sum(image_rows, axis=1),
        jnp.sum(image_rows * image_rows, axis=1),
        jnp.dot(image_rows * scale_one, weight, precision=highest),
        jnp.dot(scale_one[None, :], weight, precision=highest),
        jnp.dot(final_shift[None, :], weight, precision=highest),
    )
    row_sums, squares, scaled_proj, scale_proj, shift_proj = tp_sum(terms)
    row_mean = row_sums / model_width
    inv_std = lax.rsqrt(squares / model_width - row_mean * row_mean + 1e-06)
    velocity = (
        inv_std[:, None] * (scaled_proj - row_mean[:, None] * scale_proj) + shift_proj
    )

    half_rows = IMG_DEV // 2
    is_cond = local_seq % 2 == 0
    outgoing = jnp.where(is_cond, velocity[half_rows:], velocity[:half_rows])
    partner_half = swapped(outgoing, "seq", bit_count)
    own_half = jnp.where(is_cond, velocity[:half_rows], velocity[half_rows:])
    cond_vel = jnp.where(is_cond, own_half, partner_half)
    uncond_vel = jnp.where(is_cond, partner_half, own_half)
    guided = uncond_vel + GUIDE * (cond_vel - uncond_vel)
    step_now = step_index[0]
    time_step = sigma_at(step_now + 1) - sigma_at(step_now)
    return (new_hidden, log_sums, latents + time_step * guided)


def solution(mesh):
    return jax.shard_map(
        on_device,
        mesh=mesh,
        in_specs=(
            P(("pair", "seq"), "tp"),
            P(None, ("pair", "seq")),
            P("pair"),
            P(),
            P("pair", None, None),
            P("pair", None, None),
            P(None, None, "tp"),
            P(),
            P(),
            P("tp", None),
            P("tp", None),
            P(("pair", "seq"), None),
        ),
        out_specs=(P(("pair", "seq"), "tp"), P("tp", ("pair", "seq")), P(("pair", "seq"), None)),
        check_vma=False,
    )
```

```python
import jax
import jax.numpy as jnp
from jax import lax
from jax.sharding import PartitionSpec as P

ROPE_T = 16
ROPE_H = 56
ROPE_W = 56
STEPS = 8
IMG_DEV = 512
TXT_DEV = 64


GUIDE = 3.5
SHIFT = 3.0


def swapped(block, axis, bit):
    count = lax.axis_size(axis)
    route = []
    for low in range(count):
        high = low | 1 << bit
        if high != low and high < count:
            route += [(low, high), (high, low)]
    return lax.ppermute(block, axis, route)


def seq_route(spread, move):
    count_x = spread // 2
    route = []
    for group in range(4):
        for shard in range(spread):
            dest_x, dest_z = move(shard // 2, shard % 2, count_x)
            route.append((group * spread + shard, group * spread + (dest_x % count_x) * 2 + dest_z))
    return route


def rope_tables(ids_block):
    angle_parts = []
    for axis_pos, rope_width in ((0, ROPE_T), (1, ROPE_H), (2, ROPE_W)):
        frequencies = 10000.0 ** (-jnp.arange(0, rope_width, 2).astype(jnp.float32) / rope_width)
        angle_parts.append(ids_block[axis_pos].astype(jnp.float32)[:, None] * frequencies[None, :])
    angles = jnp.concatenate(angle_parts, axis=1)
    angles = jnp.repeat(angles, 2, axis=1)
    even = (jnp.arange(angles.shape[1]) % 2 == 0)[None, :]
    sine = jnp.sin(angles)
    return (jnp.cos(angles), jnp.where(even, -sine, sine), even)


def rotate(tensor, cosine, signed_sine, even):
    partner = jnp.where(
        even[None], jnp.roll(tensor, -1, axis=-1), jnp.roll(tensor, 1, axis=-1)
    )
    return tensor * cosine[None] + partner * signed_sine[None]


def rms_gain(tensor, gain_vec):
    return tensor * lax.rsqrt(jnp.mean(tensor * tensor, axis=-1, keepdims=True) + 1e-06) * gain_vec


def modulate(features, shift_vec, scale_vec):
    row_mean = jnp.mean(features, axis=-1, keepdims=True)
    row_var = jnp.mean(features * features, axis=-1, keepdims=True) - row_mean * row_mean
    return (features - row_mean) * lax.rsqrt(row_var + 1e-06) * (1.0 + scale_vec) + shift_vec


def sigma_at(step_now):
    time_now = 1.0 - step_now.astype(jnp.float32) / STEPS
    return SHIFT * time_now / (1.0 + (SHIFT - 1.0) * time_now)


def fold_block(state, queries, key_block, value_block, shard, text_count):
    row_max, row_sum, weighted = state
    rows_dev = key_block.shape[1]
    offset = jnp.arange(rows_dev, dtype=jnp.int32)
    text_index = shard * TXT_DEV + offset - IMG_DEV
    is_live = (offset < IMG_DEV) | (text_index < text_count)
    score_scale = queries.shape[-1] ** (-0.5)
    scores = (
        jnp.einsum("hqd,hkd->hqk", queries, key_block, preferred_element_type=jnp.float32)
        * score_scale
    )
    scores = jnp.where(is_live[None, None, :], scores, -jnp.inf)
    new_max = jnp.maximum(row_max, jnp.max(scores, axis=2))
    exps = jnp.exp(scores - new_max[:, :, None])
    decay = jnp.exp(row_max - new_max)
    row_sum = row_sum * decay + jnp.sum(exps, axis=2)
    weighted = weighted * decay[:, :, None] + jnp.einsum(
        "hqk,hkd->hqd", exps.astype(jnp.bfloat16), value_block, preferred_element_type=jnp.float32
    )
    return (new_max, row_sum, weighted)


def merge_states(first, second):
    max_a, sum_a, acc_a = first
    max_b, sum_b, acc_b = second
    new_max = jnp.maximum(max_a, max_b)
    scale_a = jnp.exp(max_a - new_max)
    scale_b = jnp.exp(max_b - new_max)
    return (
        new_max,
        sum_a * scale_a + sum_b * scale_b,
        acc_a * scale_a[:, :, None] + acc_b * scale_b[:, :, None],
    )


def tp_sum(tree):
    count = lax.axis_size("tp")
    bit = 0
    while 1 << bit < count:
        far = swapped(tree, "tp", bit)
        tree = jax.tree.map(lambda a, b: a + b, tree, far)
        bit += 1
    return tree


def on_device(
    hidden,
    positions,
    lengths,
    step_index,
    layer_mod,
    final_mod,
    qkv_weight,
    q_gain,
    k_gain,
    out_weight,
    final_weight,
    latents,
):
    spread = lax.axis_size("seq") // 4
    bit_count = spread.bit_length() - 1
    seq_pos = lax.axis_index("seq")
    local_seq = seq_pos // spread
    shard_pos = seq_pos % spread
    count_x = spread // 2
    my_x = shard_pos // 2
    my_z = shard_pos % 2
    tp_pos = lax.axis_index("tp")
    local_width = hidden.shape[1]
    gathered = lax.all_gather(hidden, "tp", axis=1, tiled=True)
    model_width = gathered.shape[1]
    rows_dev = gathered.shape[0]
    layer_terms = lax.dynamic_index_in_dim(layer_mod, local_seq, 0, keepdims=False)
    text_count = lax.dynamic_index_in_dim(lengths, local_seq, 0, keepdims=False)
    modulated = modulate(gathered.astype(jnp.float32), layer_terms[0], layer_terms[1]).astype(
        jnp.bfloat16
    )
    head_dim = q_gain.shape[0]
    head_cols = qkv_weight.shape[2]
    heads_here = head_cols // head_dim
    weight4 = qkv_weight.reshape(model_width, 3, heads_here, head_dim)
    projected = jnp.einsum(
        "rf,fchd->chrd", modulated, weight4, preferred_element_type=jnp.float32
    )
    cosine, signed_sine, even = rope_tables(positions)
    queries = rotate(rms_gain(projected[0], q_gain), cosine, signed_sine, even).astype(jnp.bfloat16)
    key_rot = rotate(rms_gain(projected[1], k_gain), cosine, signed_sine, even).astype(jnp.bfloat16)
    values = projected[2].astype(jnp.bfloat16)
    own = jnp.stack([key_rot, values])

    to_left = seq_route(spread, lambda x, z, n: (x - 1, z))
    to_right = seq_route(spread, lambda x, z, n: (x + 1, z))
    to_other_z = seq_route(spread, lambda x, z, n: (x, 1 - z))

    def shard_of(x, z):
        return (x % count_x) * 2 + z

    got_z = lax.ppermute(own, "seq", to_other_z)
    got_right = lax.ppermute(own, "seq", to_left)
    got_left = lax.ppermute(own, "seq", to_right)

    softmax_state = (
        jnp.full((heads_here, rows_dev), -jnp.inf, jnp.float32),
        jnp.zeros((heads_here, rows_dev), jnp.float32),
        jnp.zeros((heads_here, rows_dev, head_dim), jnp.float32),
    )
    softmax_state = fold_block(softmax_state, queries, own[0], own[1], shard_pos, text_count)

    z_from_right, far_keys = lax.ppermute((got_z, got_right[0]), "seq", to_left)
    z_from_left, far_values = lax.ppermute((got_z, got_left[1]), "seq", to_right)

    other_z = 1 - my_z
    softmax_state = fold_block(
        softmax_state, queries, got_z[0], got_z[1], shard_of(my_x, other_z), text_count
    )
    softmax_state = fold_block(
        softmax_state, queries, got_right[0], got_right[1], shard_of(my_x + 1, my_z), text_count
    )
    softmax_state = fold_block(
        softmax_state, queries, got_left[0], got_left[1], shard_of(my_x - 1, my_z), text_count
    )

    far_z_keys = lax.ppermute(z_from_right[0], "seq", to_left)
    far_z_values = lax.ppermute(z_from_left[1], "seq", to_right)

    late_state = (
        jnp.full((heads_here, rows_dev), -jnp.inf, jnp.float32),
        jnp.zeros((heads_here, rows_dev), jnp.float32),
        jnp.zeros((heads_here, rows_dev, head_dim), jnp.float32),
    )
    late_state = fold_block(
        late_state, queries, far_keys, far_values, shard_of(my_x + 2, my_z), text_count
    )
    late_state = fold_block(
        late_state, queries, z_from_right[0], z_from_right[1], shard_of(my_x + 1, other_z), text_count
    )
    late_state = fold_block(
        late_state, queries, z_from_left[0], z_from_left[1], shard_of(my_x - 1, other_z), text_count
    )
    softmax_state = fold_block(
        softmax_state, queries, far_z_keys, far_z_values, shard_of(my_x + 2, other_z), text_count
    )
    softmax_state = merge_states(softmax_state, late_state)

    row_max, row_sum, weighted = softmax_state
    attended = (weighted / row_sum[:, :, None]).astype(jnp.bfloat16)
    log_sums = row_max + jnp.log(row_sum)
    tp_count = lax.axis_size("tp")
    hold = jnp.minimum(jnp.abs(queries[0, 0, 0]), 0).astype(out_weight.dtype)
    attended_parts = [attended]
    weight_parts = [lax.dynamic_slice_in_dim(out_weight, tp_pos * local_width, local_width, 1)]
    for shift in range(1, tp_count):
        route = [(src, (src + shift) % tp_count) for src in range(tp_count)]
        dest = (tp_pos + shift) % tp_count
        weight_send = lax.dynamic_slice_in_dim(out_weight, dest * local_width, local_width, 1)
        weight_parts.append(lax.ppermute(weight_send + hold, "tp", route))
        attended_parts.append(lax.ppermute(attended, "tp", route))
    all_attended = jnp.stack(attended_parts)
    all_weights = jnp.stack(weight_parts).reshape(tp_count, heads_here, head_dim, local_width)
    update = jnp.einsum(
        "khrd,khdf->rf", all_attended, all_weights, preferred_element_type=jnp.float32
    )
    gate_slice = lax.dynamic_slice_in_dim(layer_terms[2], tp_pos * local_width, local_width, 0)
    new_hidden = (hidden.astype(jnp.float32) + gate_slice * update).astype(jnp.bfloat16)

    final_terms = lax.dynamic_index_in_dim(final_mod, local_seq, 0, keepdims=False)
    final_shift = lax.dynamic_slice_in_dim(final_terms[0], tp_pos * local_width, local_width, 0)
    final_scale = lax.dynamic_slice_in_dim(final_terms[1], tp_pos * local_width, local_width, 0)
    image_rows = new_hidden[:IMG_DEV].astype(jnp.float32)
    weight = final_weight.astype(jnp.float32)
    scale_one = 1.0 + final_scale
    highest = lax.Precision.HIGHEST
    terms = (
        jnp.sum(image_rows, axis=1),
        jnp.sum(image_rows * image_rows, axis=1),
        jnp.dot(image_rows * scale_one, weight, precision=highest),
        jnp.dot(scale_one[None, :], weight, precision=highest),
        jnp.dot(final_shift[None, :], weight, precision=highest),
    )
    row_sums, squares, scaled_proj, scale_proj, shift_proj = tp_sum(terms)
    row_mean = row_sums / model_width
    inv_std = lax.rsqrt(squares / model_width - row_mean * row_mean + 1e-06)
    velocity = (
        inv_std[:, None] * (scaled_proj - row_mean[:, None] * scale_proj) + shift_proj
    )

    half_rows = IMG_DEV // 2
    is_cond = local_seq % 2 == 0
    outgoing = jnp.where(is_cond, velocity[half_rows:], velocity[:half_rows])
    partner_half = swapped(outgoing, "seq", bit_count)
    own_half = jnp.where(is_cond, velocity[:half_rows], velocity[half_rows:])
    cond_vel = jnp.where(is_cond, own_half, partner_half)
    uncond_vel = jnp.where(is_cond, partner_half, own_half)
    guided = uncond_vel + GUIDE * (cond_vel - uncond_vel)
    step_now = step_index[0]
    time_step = sigma_at(step_now + 1) - sigma_at(step_now)
    return (new_hidden, log_sums, latents + time_step * guided)


def solution(mesh):
    return jax.shard_map(
        on_device,
        mesh=mesh,
        in_specs=(
            P(("pair", "seq"), "tp"),
            P(None, ("pair", "seq")),
            P("pair"),
            P(),
            P("pair", None, None),
            P("pair", None, None),
            P(None, None, "tp"),
            P(),
            P(),
            P("tp", None),
            P("tp", None),
            P(("pair", "seq"), None),
        ),
        out_specs=(P(("pair", "seq"), "tp"), P("tp", ("pair", "seq")), P(("pair", "seq"), None)),
        check_vma=False,
    )
```

```python
import jax
import jax.numpy as jnp
from jax import lax
from jax.sharding import PartitionSpec as P

ROPE_T = 16
ROPE_H = 56
ROPE_W = 56
STEPS = 8
IMG_DEV = 512
TXT_DEV = 64


GUIDE = 3.5
SHIFT = 3.0


def swapped(block, axis, bit):
    count = lax.axis_size(axis)
    route = []
    for low in range(count):
        high = low | 1 << bit
        if high != low and high < count:
            route += [(low, high), (high, low)]
    return lax.ppermute(block, axis, route)


def seq_route(spread, move):
    count_x = spread // 2
    route = []
    for group in range(4):
        for shard in range(spread):
            dest_x, dest_z = move(shard // 2, shard % 2, count_x)
            route.append((group * spread + shard, group * spread + (dest_x % count_x) * 2 + dest_z))
    return route


def rope_tables(ids_block):
    angle_parts = []
    for axis_pos, rope_width in ((0, ROPE_T), (1, ROPE_H), (2, ROPE_W)):
        frequencies = 10000.0 ** (-jnp.arange(0, rope_width, 2).astype(jnp.float32) / rope_width)
        angle_parts.append(ids_block[axis_pos].astype(jnp.float32)[:, None] * frequencies[None, :])
    angles = jnp.concatenate(angle_parts, axis=1)
    angles = jnp.repeat(angles, 2, axis=1)
    even = (jnp.arange(angles.shape[1]) % 2 == 0)[None, :]
    sine = jnp.sin(angles)
    return (jnp.cos(angles), jnp.where(even, -sine, sine), even)


def rotate(tensor, cosine, signed_sine, even):
    partner = jnp.where(
        even[None], jnp.roll(tensor, -1, axis=-1), jnp.roll(tensor, 1, axis=-1)
    )
    return tensor * cosine[None] + partner * signed_sine[None]


def rms_gain(tensor, gain_vec):
    return tensor * lax.rsqrt(jnp.mean(tensor * tensor, axis=-1, keepdims=True) + 1e-06) * gain_vec


def modulate(features, shift_vec, scale_vec):
    row_mean = jnp.mean(features, axis=-1, keepdims=True)
    row_var = jnp.mean(features * features, axis=-1, keepdims=True) - row_mean * row_mean
    return (features - row_mean) * lax.rsqrt(row_var + 1e-06) * (1.0 + scale_vec) + shift_vec


def sigma_at(step_now):
    time_now = 1.0 - step_now.astype(jnp.float32) / STEPS
    return SHIFT * time_now / (1.0 + (SHIFT - 1.0) * time_now)


def fold_block(state, queries, key_block, value_block, shard, text_count):
    row_max, row_sum, weighted = state
    rows_dev = key_block.shape[1]
    offset = jnp.arange(rows_dev, dtype=jnp.int32)
    text_index = shard * TXT_DEV + offset - IMG_DEV
    is_live = (offset < IMG_DEV) | (text_index < text_count)
    score_scale = queries.shape[-1] ** (-0.5)
    scores = (
        jnp.einsum("hqd,hkd->hqk", queries, key_block, preferred_element_type=jnp.float32)
        * score_scale
    )
    scores = jnp.where(is_live[None, None, :], scores, -jnp.inf)
    new_max = jnp.maximum(row_max, jnp.max(scores, axis=2))
    exps = jnp.exp(scores - new_max[:, :, None])
    decay = jnp.exp(row_max - new_max)
    row_sum = row_sum * decay + jnp.sum(exps, axis=2)
    weighted = weighted * decay[:, :, None] + jnp.einsum(
        "hqk,hkd->hqd", exps.astype(jnp.bfloat16), value_block, preferred_element_type=jnp.float32
    )
    return (new_max, row_sum, weighted)


def merge_states(first, second):
    max_a, sum_a, acc_a = first
    max_b, sum_b, acc_b = second
    new_max = jnp.maximum(max_a, max_b)
    scale_a = jnp.exp(max_a - new_max)
    scale_b = jnp.exp(max_b - new_max)
    return (
        new_max,
        sum_a * scale_a + sum_b * scale_b,
        acc_a * scale_a[:, :, None] + acc_b * scale_b[:, :, None],
    )


def tp_sum(tree):
    count = lax.axis_size("tp")
    bit = 0
    while 1 << bit < count:
        far = swapped(tree, "tp", bit)
        tree = jax.tree.map(lambda a, b: a + b, tree, far)
        bit += 1
    return tree


def on_device(
    hidden,
    positions,
    lengths,
    step_index,
    layer_mod,
    final_mod,
    qkv_weight,
    q_gain,
    k_gain,
    out_weight,
    final_weight,
    latents,
):
    spread = lax.axis_size("seq") // 4
    bit_count = spread.bit_length() - 1
    seq_pos = lax.axis_index("seq")
    local_seq = seq_pos // spread
    shard_pos = seq_pos % spread
    count_x = spread // 2
    my_x = shard_pos // 2
    my_z = shard_pos % 2
    tp_pos = lax.axis_index("tp")
    local_width = hidden.shape[1]
    tp_count = lax.axis_size("tp")
    parts = [hidden]
    for shift in range(1, tp_count):
        route = [(src, (src + shift) % tp_count) for src in range(tp_count)]
        parts.append(lax.ppermute(hidden, "tp", route))
    stacked = jnp.stack(parts)
    gathered = jnp.concatenate(
        [
            lax.dynamic_index_in_dim(stacked, (tp_pos - owner) % tp_count, 0, keepdims=False)
            for owner in range(tp_count)
        ],
        axis=1,
    )
    model_width = gathered.shape[1]
    rows_dev = gathered.shape[0]
    layer_terms = lax.dynamic_index_in_dim(layer_mod, local_seq, 0, keepdims=False)
    text_count = lax.dynamic_index_in_dim(lengths, local_seq, 0, keepdims=False)
    modulated = modulate(gathered.astype(jnp.float32), layer_terms[0], layer_terms[1]).astype(
        jnp.bfloat16
    )
    head_dim = q_gain.shape[0]
    head_cols = qkv_weight.shape[2]
    heads_here = head_cols // head_dim
    weight4 = qkv_weight.reshape(model_width, 3, heads_here, head_dim)
    projected = jnp.einsum(
        "rf,fchd->chrd", modulated, weight4, preferred_element_type=jnp.float32
    )
    cosine, signed_sine, even = rope_tables(positions)
    queries = rotate(rms_gain(projected[0], q_gain), cosine, signed_sine, even).astype(jnp.bfloat16)
    key_rot = rotate(rms_gain(projected[1], k_gain), cosine, signed_sine, even).astype(jnp.bfloat16)
    values = projected[2].astype(jnp.bfloat16)
    own = jnp.stack([key_rot, values])

    to_left = seq_route(spread, lambda x, z, n: (x - 1, z))
    to_right = seq_route(spread, lambda x, z, n: (x + 1, z))
    to_other_z = seq_route(spread, lambda x, z, n: (x, 1 - z))

    def shard_of(x, z):
        return (x % count_x) * 2 + z

    got_z = lax.ppermute(own, "seq", to_other_z)
    got_right = lax.ppermute(own, "seq", to_left)
    got_left = lax.ppermute(own, "seq", to_right)

    softmax_state = (
        jnp.full((heads_here, rows_dev), -jnp.inf, jnp.float32),
        jnp.zeros((heads_here, rows_dev), jnp.float32),
        jnp.zeros((heads_here, rows_dev, head_dim), jnp.float32),
    )
    softmax_state = fold_block(softmax_state, queries, own[0], own[1], shard_pos, text_count)

    z_from_right, far_keys = lax.ppermute((got_z, got_right[0]), "seq", to_left)
    z_from_left, far_values = lax.ppermute((got_z, got_left[1]), "seq", to_right)

    other_z = 1 - my_z
    softmax_state = fold_block(
        softmax_state, queries, got_z[0], got_z[1], shard_of(my_x, other_z), text_count
    )
    softmax_state = fold_block(
        softmax_state, queries, got_right[0], got_right[1], shard_of(my_x + 1, my_z), text_count
    )
    softmax_state = fold_block(
        softmax_state, queries, got_left[0], got_left[1], shard_of(my_x - 1, my_z), text_count
    )

    far_z_keys = lax.ppermute(z_from_right[0], "seq", to_left)
    far_z_values = lax.ppermute(z_from_left[1], "seq", to_right)

    late_state = (
        jnp.full((heads_here, rows_dev), -jnp.inf, jnp.float32),
        jnp.zeros((heads_here, rows_dev), jnp.float32),
        jnp.zeros((heads_here, rows_dev, head_dim), jnp.float32),
    )
    late_state = fold_block(
        late_state, queries, far_keys, far_values, shard_of(my_x + 2, my_z), text_count
    )
    late_state = fold_block(
        late_state, queries, z_from_right[0], z_from_right[1], shard_of(my_x + 1, other_z), text_count
    )
    late_state = fold_block(
        late_state, queries, z_from_left[0], z_from_left[1], shard_of(my_x - 1, other_z), text_count
    )
    softmax_state = fold_block(
        softmax_state, queries, far_z_keys, far_z_values, shard_of(my_x + 2, other_z), text_count
    )
    softmax_state = merge_states(softmax_state, late_state)

    row_max, row_sum, weighted = softmax_state
    attended = (weighted / row_sum[:, :, None]).astype(jnp.bfloat16)
    log_sums = row_max + jnp.log(row_sum)
    hold = jnp.minimum(jnp.abs(queries[0, 0, 0]), 0).astype(out_weight.dtype)
    attended_parts = [attended]
    weight_parts = [lax.dynamic_slice_in_dim(out_weight, tp_pos * local_width, local_width, 1)]
    for shift in range(1, tp_count):
        route = [(src, (src + shift) % tp_count) for src in range(tp_count)]
        dest = (tp_pos + shift) % tp_count
        weight_send = lax.dynamic_slice_in_dim(out_weight, dest * local_width, local_width, 1)
        weight_parts.append(lax.ppermute(weight_send + hold, "tp", route))
        attended_parts.append(lax.ppermute(attended, "tp", route))
    all_attended = jnp.stack(attended_parts)
    all_weights = jnp.stack(weight_parts).reshape(tp_count, heads_here, head_dim, local_width)
    update = jnp.einsum(
        "khrd,khdf->rf", all_attended, all_weights, preferred_element_type=jnp.float32
    )
    gate_slice = lax.dynamic_slice_in_dim(layer_terms[2], tp_pos * local_width, local_width, 0)
    new_hidden = (hidden.astype(jnp.float32) + gate_slice * update).astype(jnp.bfloat16)

    final_terms = lax.dynamic_index_in_dim(final_mod, local_seq, 0, keepdims=False)
    final_shift = lax.dynamic_slice_in_dim(final_terms[0], tp_pos * local_width, local_width, 0)
    final_scale = lax.dynamic_slice_in_dim(final_terms[1], tp_pos * local_width, local_width, 0)
    image_rows = new_hidden[:IMG_DEV].astype(jnp.float32)
    weight = final_weight.astype(jnp.float32)
    scale_one = 1.0 + final_scale
    highest = lax.Precision.HIGHEST
    terms = (
        jnp.sum(image_rows, axis=1),
        jnp.sum(image_rows * image_rows, axis=1),
        jnp.dot(image_rows * scale_one, weight, precision=highest),
        jnp.dot(scale_one[None, :], weight, precision=highest),
        jnp.dot(final_shift[None, :], weight, precision=highest),
    )
    row_sums, squares, scaled_proj, scale_proj, shift_proj = tp_sum(terms)
    row_mean = row_sums / model_width
    inv_std = lax.rsqrt(squares / model_width - row_mean * row_mean + 1e-06)
    velocity = (
        inv_std[:, None] * (scaled_proj - row_mean[:, None] * scale_proj) + shift_proj
    )

    half_rows = IMG_DEV // 2
    is_cond = local_seq % 2 == 0
    outgoing = jnp.where(is_cond, velocity[half_rows:], velocity[:half_rows])
    partner_half = swapped(outgoing, "seq", bit_count)
    own_half = jnp.where(is_cond, velocity[:half_rows], velocity[half_rows:])
    cond_vel = jnp.where(is_cond, own_half, partner_half)
    uncond_vel = jnp.where(is_cond, partner_half, own_half)
    guided = uncond_vel + GUIDE * (cond_vel - uncond_vel)
    step_now = step_index[0]
    time_step = sigma_at(step_now + 1) - sigma_at(step_now)
    return (new_hidden, log_sums, latents + time_step * guided)


def solution(mesh):
    return jax.shard_map(
        on_device,
        mesh=mesh,
        in_specs=(
            P(("pair", "seq"), "tp"),
            P(None, ("pair", "seq")),
            P("pair"),
            P(),
            P("pair", None, None),
            P("pair", None, None),
            P(None, None, "tp"),
            P(),
            P(),
            P("tp", None),
            P("tp", None),
            P(("pair", "seq"), None),
        ),
        out_specs=(P(("pair", "seq"), "tp"), P("tp", ("pair", "seq")), P(("pair", "seq"), None)),
        check_vma=False,
    )
```

```python
import jax
import jax.numpy as jnp
from jax import lax
from jax.sharding import PartitionSpec as P

ROPE_T = 16
ROPE_H = 56
ROPE_W = 56
STEPS = 8
IMG_DEV = 512
TXT_DEV = 64


GUIDE = 3.5
SHIFT = 3.0


def swapped(block, axis, bit):
    count = lax.axis_size(axis)
    route = []
    for low in range(count):
        high = low | 1 << bit
        if high != low and high < count:
            route += [(low, high), (high, low)]
    return lax.ppermute(block, axis, route)


def seq_route(spread, move):
    count_x = spread // 2
    route = []
    for group in range(4):
        for shard in range(spread):
            dest_x, dest_z = move(shard // 2, shard % 2, count_x)
            route.append((group * spread + shard, group * spread + (dest_x % count_x) * 2 + dest_z))
    return route


def rope_tables(ids_block):
    angle_parts = []
    for axis_pos, rope_width in ((0, ROPE_T), (1, ROPE_H), (2, ROPE_W)):
        frequencies = 10000.0 ** (-jnp.arange(0, rope_width, 2).astype(jnp.float32) / rope_width)
        angle_parts.append(ids_block[axis_pos].astype(jnp.float32)[:, None] * frequencies[None, :])
    angles = jnp.concatenate(angle_parts, axis=1)
    angles = jnp.repeat(angles, 2, axis=1)
    even = (jnp.arange(angles.shape[1]) % 2 == 0)[None, :]
    sine = jnp.sin(angles)
    return (jnp.cos(angles), jnp.where(even, -sine, sine), even)


def rotate(tensor, cosine, signed_sine, even):
    partner = jnp.where(
        even[None], jnp.roll(tensor, -1, axis=-1), jnp.roll(tensor, 1, axis=-1)
    )
    return tensor * cosine[None] + partner * signed_sine[None]


def rms_gain(tensor, gain_vec):
    return tensor * lax.rsqrt(jnp.mean(tensor * tensor, axis=-1, keepdims=True) + 1e-06) * gain_vec


def modulate(features, shift_vec, scale_vec):
    row_mean = jnp.mean(features, axis=-1, keepdims=True)
    row_var = jnp.mean(features * features, axis=-1, keepdims=True) - row_mean * row_mean
    return (features - row_mean) * lax.rsqrt(row_var + 1e-06) * (1.0 + scale_vec) + shift_vec


def sigma_at(step_now):
    time_now = 1.0 - step_now.astype(jnp.float32) / STEPS
    return SHIFT * time_now / (1.0 + (SHIFT - 1.0) * time_now)


def fold_block(state, queries, key_block, value_block, shard, text_count):
    row_max, row_sum, weighted = state
    rows_dev = key_block.shape[1]
    offset = jnp.arange(rows_dev, dtype=jnp.int32)
    text_index = shard * TXT_DEV + offset - IMG_DEV
    is_live = (offset < IMG_DEV) | (text_index < text_count)
    score_scale = queries.shape[-1] ** (-0.5)
    scores = (
        jnp.einsum("hqd,hkd->hqk", queries, key_block, preferred_element_type=jnp.float32)
        * score_scale
    )
    scores = jnp.where(is_live[None, None, :], scores, -jnp.inf)
    new_max = jnp.maximum(row_max, jnp.max(scores, axis=2))
    exps = jnp.exp(scores - new_max[:, :, None])
    decay = jnp.exp(row_max - new_max)
    row_sum = row_sum * decay + jnp.sum(exps, axis=2)
    weighted = weighted * decay[:, :, None] + jnp.einsum(
        "hqk,hkd->hqd", exps.astype(jnp.bfloat16), value_block, preferred_element_type=jnp.float32
    )
    return (new_max, row_sum, weighted)


def merge_states(first, second):
    max_a, sum_a, acc_a = first
    max_b, sum_b, acc_b = second
    new_max = jnp.maximum(max_a, max_b)
    scale_a = jnp.exp(max_a - new_max)
    scale_b = jnp.exp(max_b - new_max)
    return (
        new_max,
        sum_a * scale_a + sum_b * scale_b,
        acc_a * scale_a[:, :, None] + acc_b * scale_b[:, :, None],
    )


def tp_sum(tree):
    count = lax.axis_size("tp")
    bit = 0
    while 1 << bit < count:
        far = swapped(tree, "tp", bit)
        tree = jax.tree.map(lambda a, b: a + b, tree, far)
        bit += 1
    return tree


def on_device(
    hidden,
    positions,
    lengths,
    step_index,
    layer_mod,
    final_mod,
    qkv_weight,
    q_gain,
    k_gain,
    out_weight,
    final_weight,
    latents,
):
    spread = lax.axis_size("seq") // 4
    bit_count = spread.bit_length() - 1
    seq_pos = lax.axis_index("seq")
    local_seq = seq_pos // spread
    shard_pos = seq_pos % spread
    count_x = spread // 2
    my_x = shard_pos // 2
    my_z = shard_pos % 2
    tp_pos = lax.axis_index("tp")
    local_width = hidden.shape[1]
    tp_count = lax.axis_size("tp")
    parts = [hidden]
    weight_parts = [lax.dynamic_slice_in_dim(out_weight, tp_pos * local_width, local_width, 1)]
    for shift in range(1, tp_count):
        route = [(src, (src + shift) % tp_count) for src in range(tp_count)]
        dest = (tp_pos + shift) % tp_count
        weight_send = lax.dynamic_slice_in_dim(out_weight, dest * local_width, local_width, 1)
        hidden_part, weight_part = lax.ppermute((hidden, weight_send), "tp", route)
        parts.append(hidden_part)
        weight_parts.append(weight_part)
    stacked = jnp.stack(parts)
    gathered = jnp.concatenate(
        [
            lax.dynamic_index_in_dim(stacked, (tp_pos - owner) % tp_count, 0, keepdims=False)
            for owner in range(tp_count)
        ],
        axis=1,
    )
    model_width = gathered.shape[1]
    rows_dev = gathered.shape[0]
    layer_terms = lax.dynamic_index_in_dim(layer_mod, local_seq, 0, keepdims=False)
    text_count = lax.dynamic_index_in_dim(lengths, local_seq, 0, keepdims=False)
    modulated = modulate(gathered.astype(jnp.float32), layer_terms[0], layer_terms[1]).astype(
        jnp.bfloat16
    )
    head_dim = q_gain.shape[0]
    head_cols = qkv_weight.shape[2]
    heads_here = head_cols // head_dim
    weight4 = qkv_weight.reshape(model_width, 3, heads_here, head_dim)
    projected = jnp.einsum(
        "rf,fchd->chrd", modulated, weight4, preferred_element_type=jnp.float32
    )
    cosine, signed_sine, even = rope_tables(positions)
    queries = rotate(rms_gain(projected[0], q_gain), cosine, signed_sine, even).astype(jnp.bfloat16)
    key_rot = rotate(rms_gain(projected[1], k_gain), cosine, signed_sine, even).astype(jnp.bfloat16)
    values = projected[2].astype(jnp.bfloat16)
    own = jnp.stack([key_rot, values])

    to_left = seq_route(spread, lambda x, z, n: (x - 1, z))
    to_right = seq_route(spread, lambda x, z, n: (x + 1, z))
    to_other_z = seq_route(spread, lambda x, z, n: (x, 1 - z))

    def shard_of(x, z):
        return (x % count_x) * 2 + z

    got_z = lax.ppermute(own, "seq", to_other_z)
    got_right = lax.ppermute(own, "seq", to_left)
    got_left = lax.ppermute(own, "seq", to_right)

    softmax_state = (
        jnp.full((heads_here, rows_dev), -jnp.inf, jnp.float32),
        jnp.zeros((heads_here, rows_dev), jnp.float32),
        jnp.zeros((heads_here, rows_dev, head_dim), jnp.float32),
    )
    softmax_state = fold_block(softmax_state, queries, own[0], own[1], shard_pos, text_count)

    z_from_right, far_keys = lax.ppermute((got_z, got_right[0]), "seq", to_left)
    z_from_left, far_values = lax.ppermute((got_z, got_left[1]), "seq", to_right)

    other_z = 1 - my_z
    softmax_state = fold_block(
        softmax_state, queries, got_z[0], got_z[1], shard_of(my_x, other_z), text_count
    )
    softmax_state = fold_block(
        softmax_state, queries, got_right[0], got_right[1], shard_of(my_x + 1, my_z), text_count
    )
    softmax_state = fold_block(
        softmax_state, queries, got_left[0], got_left[1], shard_of(my_x - 1, my_z), text_count
    )

    far_z_keys = lax.ppermute(z_from_right[0], "seq", to_left)
    far_z_values = lax.ppermute(z_from_left[1], "seq", to_right)

    late_state = (
        jnp.full((heads_here, rows_dev), -jnp.inf, jnp.float32),
        jnp.zeros((heads_here, rows_dev), jnp.float32),
        jnp.zeros((heads_here, rows_dev, head_dim), jnp.float32),
    )
    late_state = fold_block(
        late_state, queries, far_keys, far_values, shard_of(my_x + 2, my_z), text_count
    )
    late_state = fold_block(
        late_state, queries, z_from_right[0], z_from_right[1], shard_of(my_x + 1, other_z), text_count
    )
    late_state = fold_block(
        late_state, queries, z_from_left[0], z_from_left[1], shard_of(my_x - 1, other_z), text_count
    )
    softmax_state = fold_block(
        softmax_state, queries, far_z_keys, far_z_values, shard_of(my_x + 2, other_z), text_count
    )
    softmax_state = merge_states(softmax_state, late_state)

    row_max, row_sum, weighted = softmax_state
    attended = (weighted / row_sum[:, :, None]).astype(jnp.bfloat16)
    log_sums = row_max + jnp.log(row_sum)
    attended_parts = [attended]
    for shift in range(1, tp_count):
        route = [(src, (src + shift) % tp_count) for src in range(tp_count)]
        attended_parts.append(lax.ppermute(attended, "tp", route))
    all_attended = jnp.stack(attended_parts)
    all_weights = jnp.stack(weight_parts).reshape(tp_count, heads_here, head_dim, local_width)
    update = jnp.einsum(
        "khrd,khdf->rf", all_attended, all_weights, preferred_element_type=jnp.float32
    )
    gate_slice = lax.dynamic_slice_in_dim(layer_terms[2], tp_pos * local_width, local_width, 0)
    new_hidden = (hidden.astype(jnp.float32) + gate_slice * update).astype(jnp.bfloat16)

    final_terms = lax.dynamic_index_in_dim(final_mod, local_seq, 0, keepdims=False)
    final_shift = lax.dynamic_slice_in_dim(final_terms[0], tp_pos * local_width, local_width, 0)
    final_scale = lax.dynamic_slice_in_dim(final_terms[1], tp_pos * local_width, local_width, 0)
    image_rows = new_hidden[:IMG_DEV].astype(jnp.float32)
    weight = final_weight.astype(jnp.float32)
    scale_one = 1.0 + final_scale
    highest = lax.Precision.HIGHEST
    terms = (
        jnp.sum(image_rows, axis=1),
        jnp.sum(image_rows * image_rows, axis=1),
        jnp.dot(image_rows * scale_one, weight, precision=highest),
        jnp.dot(scale_one[None, :], weight, precision=highest),
        jnp.dot(final_shift[None, :], weight, precision=highest),
    )
    row_sums, squares, scaled_proj, scale_proj, shift_proj = tp_sum(terms)
    row_mean = row_sums / model_width
    inv_std = lax.rsqrt(squares / model_width - row_mean * row_mean + 1e-06)
    velocity = (
        inv_std[:, None] * (scaled_proj - row_mean[:, None] * scale_proj) + shift_proj
    )

    half_rows = IMG_DEV // 2
    is_cond = local_seq % 2 == 0
    outgoing = jnp.where(is_cond, velocity[half_rows:], velocity[:half_rows])
    partner_half = swapped(outgoing, "seq", bit_count)
    own_half = jnp.where(is_cond, velocity[:half_rows], velocity[half_rows:])
    cond_vel = jnp.where(is_cond, own_half, partner_half)
    uncond_vel = jnp.where(is_cond, partner_half, own_half)
    guided = uncond_vel + GUIDE * (cond_vel - uncond_vel)
    step_now = step_index[0]
    time_step = sigma_at(step_now + 1) - sigma_at(step_now)
    return (new_hidden, log_sums, latents + time_step * guided)


def solution(mesh):
    return jax.shard_map(
        on_device,
        mesh=mesh,
        in_specs=(
            P(("pair", "seq"), "tp"),
            P(None, ("pair", "seq")),
            P("pair"),
            P(),
            P("pair", None, None),
            P("pair", None, None),
            P(None, None, "tp"),
            P(),
            P(),
            P("tp", None),
            P("tp", None),
            P(("pair", "seq"), None),
        ),
        out_specs=(P(("pair", "seq"), "tp"), P("tp", ("pair", "seq")), P(("pair", "seq"), None)),
        check_vma=False,
    )
```

```python
import jax
import jax.numpy as jnp
from jax import lax
from jax.sharding import PartitionSpec as P

ROPE_T = 16
ROPE_H = 56
ROPE_W = 56
STEPS = 8
IMG_DEV = 512
TXT_DEV = 64


GUIDE = 3.5
SHIFT = 3.0


def swapped(block, axis, bit):
    count = lax.axis_size(axis)
    route = []
    for low in range(count):
        high = low | 1 << bit
        if high != low and high < count:
            route += [(low, high), (high, low)]
    return lax.ppermute(block, axis, route)


def seq_route(spread, move):
    count_x = spread // 2
    route = []
    for group in range(4):
        for shard in range(spread):
            dest_x, dest_z = move(shard // 2, shard % 2, count_x)
            route.append((group * spread + shard, group * spread + (dest_x % count_x) * 2 + dest_z))
    return route


def rope_tables(ids_block):
    angle_parts = []
    for axis_pos, rope_width in ((0, ROPE_T), (1, ROPE_H), (2, ROPE_W)):
        frequencies = 10000.0 ** (-jnp.arange(0, rope_width, 2).astype(jnp.float32) / rope_width)
        angle_parts.append(ids_block[axis_pos].astype(jnp.float32)[:, None] * frequencies[None, :])
    angles = jnp.concatenate(angle_parts, axis=1)
    angles = jnp.repeat(angles, 2, axis=1)
    even = (jnp.arange(angles.shape[1]) % 2 == 0)[None, :]
    sine = jnp.sin(angles)
    return (jnp.cos(angles), jnp.where(even, -sine, sine), even)


def rotate(tensor, cosine, signed_sine, even):
    partner = jnp.where(
        even[None], jnp.roll(tensor, -1, axis=-1), jnp.roll(tensor, 1, axis=-1)
    )
    return tensor * cosine[None] + partner * signed_sine[None]


def rms_gain(tensor, gain_vec):
    return tensor * lax.rsqrt(jnp.mean(tensor * tensor, axis=-1, keepdims=True) + 1e-06) * gain_vec


def modulate(features, shift_vec, scale_vec):
    row_mean = jnp.mean(features, axis=-1, keepdims=True)
    row_var = jnp.mean(features * features, axis=-1, keepdims=True) - row_mean * row_mean
    return (features - row_mean) * lax.rsqrt(row_var + 1e-06) * (1.0 + scale_vec) + shift_vec


def sigma_at(step_now):
    time_now = 1.0 - step_now.astype(jnp.float32) / STEPS
    return SHIFT * time_now / (1.0 + (SHIFT - 1.0) * time_now)


def fold_block(state, queries, key_block, value_block, shard, text_count):
    row_max, row_sum, weighted = state
    rows_dev = key_block.shape[1]
    offset = jnp.arange(rows_dev, dtype=jnp.int32)
    text_index = shard * TXT_DEV + offset - IMG_DEV
    is_live = (offset < IMG_DEV) | (text_index < text_count)
    score_scale = queries.shape[-1] ** (-0.5)
    scores = (
        jnp.einsum("hqd,hkd->hqk", queries, key_block, preferred_element_type=jnp.float32)
        * score_scale
    )
    scores = jnp.where(is_live[None, None, :], scores, -jnp.inf)
    new_max = jnp.maximum(row_max, jnp.max(scores, axis=2))
    exps = jnp.exp(scores - new_max[:, :, None])
    decay = jnp.exp(row_max - new_max)
    row_sum = row_sum * decay + jnp.sum(exps, axis=2)
    weighted = weighted * decay[:, :, None] + jnp.einsum(
        "hqk,hkd->hqd", exps.astype(jnp.bfloat16), value_block, preferred_element_type=jnp.float32
    )
    return (new_max, row_sum, weighted)


def fold_group(state, queries, blocks, text_count):
    rows = blocks[0][0].shape[1]
    offset = jnp.arange(rows, dtype=jnp.int32)
    is_live = jnp.concatenate(
        [(offset < IMG_DEV) | (shard * TXT_DEV + offset - IMG_DEV < text_count) for _, _, shard in blocks]
    )
    key_rows = jnp.concatenate([blk[0] for blk in blocks], axis=1)
    value_rows = jnp.concatenate([blk[1] for blk in blocks], axis=1)
    row_max, row_sum, weighted = state
    score_scale = queries.shape[-1] ** (-0.5)
    scores = (
        jnp.einsum("hqd,hkd->hqk", queries, key_rows, preferred_element_type=jnp.float32)
        * score_scale
    )
    scores = jnp.where(is_live[None, None, :], scores, -jnp.inf)
    new_max = jnp.maximum(row_max, jnp.max(scores, axis=2))
    exps = jnp.exp(scores - new_max[:, :, None])
    decay = jnp.exp(row_max - new_max)
    row_sum = row_sum * decay + jnp.sum(exps, axis=2)
    weighted = weighted * decay[:, :, None] + jnp.einsum(
        "hqk,hkd->hqd", exps.astype(jnp.bfloat16), value_rows, preferred_element_type=jnp.float32
    )
    return (new_max, row_sum, weighted)


def merge_states(first, second):
    max_a, sum_a, acc_a = first
    max_b, sum_b, acc_b = second
    new_max = jnp.maximum(max_a, max_b)
    scale_a = jnp.exp(max_a - new_max)
    scale_b = jnp.exp(max_b - new_max)
    return (
        new_max,
        sum_a * scale_a + sum_b * scale_b,
        acc_a * scale_a[:, :, None] + acc_b * scale_b[:, :, None],
    )


def tp_sum(tree):
    count = lax.axis_size("tp")
    bit = 0
    while 1 << bit < count:
        far = swapped(tree, "tp", bit)
        tree = jax.tree.map(lambda a, b: a + b, tree, far)
        bit += 1
    return tree


def on_device(
    hidden,
    positions,
    lengths,
    step_index,
    layer_mod,
    final_mod,
    qkv_weight,
    q_gain,
    k_gain,
    out_weight,
    final_weight,
    latents,
):
    spread = lax.axis_size("seq") // 4
    bit_count = spread.bit_length() - 1
    seq_pos = lax.axis_index("seq")
    local_seq = seq_pos // spread
    shard_pos = seq_pos % spread
    count_x = spread // 2
    my_x = shard_pos // 2
    my_z = shard_pos % 2
    tp_pos = lax.axis_index("tp")
    local_width = hidden.shape[1]
    tp_count = lax.axis_size("tp")
    parts = [hidden]
    for shift in range(1, tp_count):
        route = [(src, (src + shift) % tp_count) for src in range(tp_count)]
        parts.append(lax.ppermute(hidden, "tp", route))
    stacked = jnp.stack(parts)
    gathered = jnp.concatenate(
        [
            lax.dynamic_index_in_dim(stacked, (tp_pos - owner) % tp_count, 0, keepdims=False)
            for owner in range(tp_count)
        ],
        axis=1,
    )
    model_width = gathered.shape[1]
    rows_dev = gathered.shape[0]
    layer_terms = lax.dynamic_index_in_dim(layer_mod, local_seq, 0, keepdims=False)
    text_count = lax.dynamic_index_in_dim(lengths, local_seq, 0, keepdims=False)
    modulated = modulate(gathered.astype(jnp.float32), layer_terms[0], layer_terms[1]).astype(
        jnp.bfloat16
    )
    head_dim = q_gain.shape[0]
    head_cols = qkv_weight.shape[2]
    heads_here = head_cols // head_dim
    weight4 = qkv_weight.reshape(model_width, 3, heads_here, head_dim)
    projected = jnp.einsum(
        "rf,fchd->chrd", modulated, weight4, preferred_element_type=jnp.float32
    )
    cosine, signed_sine, even = rope_tables(positions)
    queries = rotate(rms_gain(projected[0], q_gain), cosine, signed_sine, even).astype(jnp.bfloat16)
    key_rot = rotate(rms_gain(projected[1], k_gain), cosine, signed_sine, even).astype(jnp.bfloat16)
    values = projected[2].astype(jnp.bfloat16)
    own = jnp.stack([key_rot, values])

    to_left = seq_route(spread, lambda x, z, n: (x - 1, z))
    to_right = seq_route(spread, lambda x, z, n: (x + 1, z))
    to_other_z = seq_route(spread, lambda x, z, n: (x, 1 - z))

    def shard_of(x, z):
        return (x % count_x) * 2 + z

    got_z = lax.ppermute(own, "seq", to_other_z)
    got_right = lax.ppermute(own, "seq", to_left)
    got_left = lax.ppermute(own, "seq", to_right)

    softmax_state = (
        jnp.full((heads_here, rows_dev), -jnp.inf, jnp.float32),
        jnp.zeros((heads_here, rows_dev), jnp.float32),
        jnp.zeros((heads_here, rows_dev, head_dim), jnp.float32),
    )
    softmax_state = fold_block(softmax_state, queries, own[0], own[1], shard_pos, text_count)

    z_from_right, far_keys = lax.ppermute((got_z, got_right[0]), "seq", to_left)
    z_from_left, far_values = lax.ppermute((got_z, got_left[1]), "seq", to_right)

    other_z = 1 - my_z
    softmax_state = fold_group(
        softmax_state,
        queries,
        [
            (got_z[0], got_z[1], shard_of(my_x, other_z)),
            (got_right[0], got_right[1], shard_of(my_x + 1, my_z)),
            (got_left[0], got_left[1], shard_of(my_x - 1, my_z)),
        ],
        text_count,
    )

    far_z_keys = lax.ppermute(z_from_right[0], "seq", to_left)
    far_z_values = lax.ppermute(z_from_left[1], "seq", to_right)

    late_state = (
        jnp.full((heads_here, rows_dev), -jnp.inf, jnp.float32),
        jnp.zeros((heads_here, rows_dev), jnp.float32),
        jnp.zeros((heads_here, rows_dev, head_dim), jnp.float32),
    )
    late_state = fold_group(
        late_state,
        queries,
        [
            (far_keys, far_values, shard_of(my_x + 2, my_z)),
            (z_from_right[0], z_from_right[1], shard_of(my_x + 1, other_z)),
            (z_from_left[0], z_from_left[1], shard_of(my_x - 1, other_z)),
        ],
        text_count,
    )
    softmax_state = fold_block(
        softmax_state, queries, far_z_keys, far_z_values, shard_of(my_x + 2, other_z), text_count
    )
    softmax_state = merge_states(softmax_state, late_state)

    row_max, row_sum, weighted = softmax_state
    attended = (weighted / row_sum[:, :, None]).astype(jnp.bfloat16)
    log_sums = row_max + jnp.log(row_sum)
    hold = jnp.minimum(jnp.abs(queries[0, 0, 0]), 0).astype(out_weight.dtype)
    attended_parts = [attended]
    weight_parts = [lax.dynamic_slice_in_dim(out_weight, tp_pos * local_width, local_width, 1)]
    for shift in range(1, tp_count):
        route = [(src, (src + shift) % tp_count) for src in range(tp_count)]
        dest = (tp_pos + shift) % tp_count
        weight_send = lax.dynamic_slice_in_dim(out_weight, dest * local_width, local_width, 1)
        weight_parts.append(lax.ppermute(weight_send + hold, "tp", route))
        attended_parts.append(lax.ppermute(attended, "tp", route))
    all_attended = jnp.stack(attended_parts)
    all_weights = jnp.stack(weight_parts).reshape(tp_count, heads_here, head_dim, local_width)
    update = jnp.einsum(
        "khrd,khdf->rf", all_attended, all_weights, preferred_element_type=jnp.float32
    )
    gate_slice = lax.dynamic_slice_in_dim(layer_terms[2], tp_pos * local_width, local_width, 0)
    new_hidden = (hidden.astype(jnp.float32) + gate_slice * update).astype(jnp.bfloat16)

    final_terms = lax.dynamic_index_in_dim(final_mod, local_seq, 0, keepdims=False)
    final_shift = lax.dynamic_slice_in_dim(final_terms[0], tp_pos * local_width, local_width, 0)
    final_scale = lax.dynamic_slice_in_dim(final_terms[1], tp_pos * local_width, local_width, 0)
    image_rows = new_hidden[:IMG_DEV].astype(jnp.float32)
    weight = final_weight.astype(jnp.float32)
    scale_one = 1.0 + final_scale
    highest = lax.Precision.HIGHEST
    terms = (
        jnp.sum(image_rows, axis=1),
        jnp.sum(image_rows * image_rows, axis=1),
        jnp.dot(image_rows * scale_one, weight, precision=highest),
        jnp.dot(scale_one[None, :], weight, precision=highest),
        jnp.dot(final_shift[None, :], weight, precision=highest),
    )
    row_sums, squares, scaled_proj, scale_proj, shift_proj = tp_sum(terms)
    row_mean = row_sums / model_width
    inv_std = lax.rsqrt(squares / model_width - row_mean * row_mean + 1e-06)
    velocity = (
        inv_std[:, None] * (scaled_proj - row_mean[:, None] * scale_proj) + shift_proj
    )

    half_rows = IMG_DEV // 2
    is_cond = local_seq % 2 == 0
    outgoing = jnp.where(is_cond, velocity[half_rows:], velocity[:half_rows])
    partner_half = swapped(outgoing, "seq", bit_count)
    own_half = jnp.where(is_cond, velocity[:half_rows], velocity[half_rows:])
    cond_vel = jnp.where(is_cond, own_half, partner_half)
    uncond_vel = jnp.where(is_cond, partner_half, own_half)
    guided = uncond_vel + GUIDE * (cond_vel - uncond_vel)
    step_now = step_index[0]
    time_step = sigma_at(step_now + 1) - sigma_at(step_now)
    return (new_hidden, log_sums, latents + time_step * guided)


def solution(mesh):
    return jax.shard_map(
        on_device,
        mesh=mesh,
        in_specs=(
            P(("pair", "seq"), "tp"),
            P(None, ("pair", "seq")),
            P("pair"),
            P(),
            P("pair", None, None),
            P("pair", None, None),
            P(None, None, "tp"),
            P(),
            P(),
            P("tp", None),
            P("tp", None),
            P(("pair", "seq"), None),
        ),
        out_specs=(P(("pair", "seq"), "tp"), P("tp", ("pair", "seq")), P(("pair", "seq"), None)),
        check_vma=False,
    )
```

```python
import jax
import jax.numpy as jnp
from jax import lax
from jax.sharding import PartitionSpec as P

ROPE_T = 16
ROPE_H = 56
ROPE_W = 56
STEPS = 8
IMG_DEV = 512
TXT_DEV = 64


GUIDE = 3.5
SHIFT = 3.0


def swapped(block, axis, bit):
    count = lax.axis_size(axis)
    route = []
    for low in range(count):
        high = low | 1 << bit
        if high != low and high < count:
            route += [(low, high), (high, low)]
    return lax.ppermute(block, axis, route)


def seq_route(spread, move):
    count_x = spread // 2
    route = []
    for group in range(4):
        for shard in range(spread):
            dest_x, dest_z = move(shard // 2, shard % 2, count_x)
            route.append((group * spread + shard, group * spread + (dest_x % count_x) * 2 + dest_z))
    return route


def rope_tables(ids_block):
    angle_parts = []
    for axis_pos, rope_width in ((0, ROPE_T), (1, ROPE_H), (2, ROPE_W)):
        frequencies = 10000.0 ** (-jnp.arange(0, rope_width, 2).astype(jnp.float32) / rope_width)
        angle_parts.append(ids_block[axis_pos].astype(jnp.float32)[:, None] * frequencies[None, :])
    angles = jnp.concatenate(angle_parts, axis=1)
    angles = jnp.repeat(angles, 2, axis=1)
    even = (jnp.arange(angles.shape[1]) % 2 == 0)[None, :]
    sine = jnp.sin(angles)
    return (jnp.cos(angles), jnp.where(even, -sine, sine), even)


def rotate(tensor, cosine, signed_sine, even):
    partner = jnp.where(
        even[None], jnp.roll(tensor, -1, axis=-1), jnp.roll(tensor, 1, axis=-1)
    )
    return tensor * cosine[None] + partner * signed_sine[None]


def rms_gain(tensor, gain_vec):
    return tensor * lax.rsqrt(jnp.mean(tensor * tensor, axis=-1, keepdims=True) + 1e-06) * gain_vec


def modulate(features, shift_vec, scale_vec):
    row_mean = jnp.mean(features, axis=-1, keepdims=True)
    row_var = jnp.mean(features * features, axis=-1, keepdims=True) - row_mean * row_mean
    return (features - row_mean) * lax.rsqrt(row_var + 1e-06) * (1.0 + scale_vec) + shift_vec


def sigma_at(step_now):
    time_now = 1.0 - step_now.astype(jnp.float32) / STEPS
    return SHIFT * time_now / (1.0 + (SHIFT - 1.0) * time_now)


def fold_block(state, queries, key_block, value_block, shard, text_count):
    row_max, row_sum, weighted = state
    rows_dev = key_block.shape[1]
    offset = jnp.arange(rows_dev, dtype=jnp.int32)
    text_index = shard * TXT_DEV + offset - IMG_DEV
    is_live = (offset < IMG_DEV) | (text_index < text_count)
    score_scale = queries.shape[-1] ** (-0.5)
    scores = (
        jnp.einsum("hqd,hkd->hqk", queries, key_block, preferred_element_type=jnp.float32)
        * score_scale
    )
    scores = jnp.where(is_live[None, None, :], scores, -jnp.inf)
    new_max = jnp.maximum(row_max, jnp.max(scores, axis=2))
    exps = jnp.exp(scores - new_max[:, :, None])
    decay = jnp.exp(row_max - new_max)
    row_sum = row_sum * decay + jnp.sum(exps, axis=2)
    weighted = weighted * decay[:, :, None] + jnp.einsum(
        "hqk,hkd->hqd", exps.astype(jnp.bfloat16), value_block, preferred_element_type=jnp.float32
    )
    return (new_max, row_sum, weighted)


def fold_group(state, queries, blocks, text_count):
    rows = blocks[0][0].shape[1]
    offset = jnp.arange(rows, dtype=jnp.int32)
    is_live = jnp.concatenate(
        [(offset < IMG_DEV) | (shard * TXT_DEV + offset - IMG_DEV < text_count) for _, _, shard in blocks]
    )
    key_rows = jnp.concatenate([blk[0] for blk in blocks], axis=1)
    value_rows = jnp.concatenate([blk[1] for blk in blocks], axis=1)
    row_max, row_sum, weighted = state
    score_scale = queries.shape[-1] ** (-0.5)
    scores = (
        jnp.einsum("hqd,hkd->hqk", queries, key_rows, preferred_element_type=jnp.float32)
        * score_scale
    )
    scores = jnp.where(is_live[None, None, :], scores, -jnp.inf)
    new_max = jnp.maximum(row_max, jnp.max(scores, axis=2))
    exps = jnp.exp(scores - new_max[:, :, None])
    decay = jnp.exp(row_max - new_max)
    row_sum = row_sum * decay + jnp.sum(exps, axis=2)
    weighted = weighted * decay[:, :, None] + jnp.einsum(
        "hqk,hkd->hqd", exps.astype(jnp.bfloat16), value_rows, preferred_element_type=jnp.float32
    )
    return (new_max, row_sum, weighted)


def merge_states(first, second):
    max_a, sum_a, acc_a = first
    max_b, sum_b, acc_b = second
    new_max = jnp.maximum(max_a, max_b)
    scale_a = jnp.exp(max_a - new_max)
    scale_b = jnp.exp(max_b - new_max)
    return (
        new_max,
        sum_a * scale_a + sum_b * scale_b,
        acc_a * scale_a[:, :, None] + acc_b * scale_b[:, :, None],
    )


def tp_sum(tree):
    count = lax.axis_size("tp")
    bit = 0
    while 1 << bit < count:
        far = swapped(tree, "tp", bit)
        tree = jax.tree.map(lambda a, b: a + b, tree, far)
        bit += 1
    return tree


def on_device(
    hidden,
    positions,
    lengths,
    step_index,
    layer_mod,
    final_mod,
    qkv_weight,
    q_gain,
    k_gain,
    out_weight,
    final_weight,
    latents,
):
    spread = lax.axis_size("seq") // 4
    bit_count = spread.bit_length() - 1
    seq_pos = lax.axis_index("seq")
    local_seq = seq_pos // spread
    shard_pos = seq_pos % spread
    count_x = spread // 2
    my_x = shard_pos // 2
    my_z = shard_pos % 2
    tp_pos = lax.axis_index("tp")
    local_width = hidden.shape[1]
    tp_count = lax.axis_size("tp")
    parts = [hidden]
    for shift in range(1, tp_count):
        route = [(src, (src + shift) % tp_count) for src in range(tp_count)]
        parts.append(lax.ppermute(hidden, "tp", route))
    stacked = jnp.stack(parts)
    gathered = jnp.concatenate(
        [
            lax.dynamic_index_in_dim(stacked, (tp_pos - owner) % tp_count, 0, keepdims=False)
            for owner in range(tp_count)
        ],
        axis=1,
    )
    model_width = gathered.shape[1]
    rows_dev = gathered.shape[0]
    layer_terms = lax.dynamic_index_in_dim(layer_mod, local_seq, 0, keepdims=False)
    text_count = lax.dynamic_index_in_dim(lengths, local_seq, 0, keepdims=False)
    modulated = modulate(gathered.astype(jnp.float32), layer_terms[0], layer_terms[1]).astype(
        jnp.bfloat16
    )
    head_dim = q_gain.shape[0]
    head_cols = qkv_weight.shape[2]
    heads_here = head_cols // head_dim
    weight4 = qkv_weight.reshape(model_width, 3, heads_here, head_dim)
    projected = jnp.einsum(
        "rf,fchd->chrd", modulated, weight4, preferred_element_type=jnp.float32
    )
    cosine, signed_sine, even = rope_tables(positions)
    queries = rotate(rms_gain(projected[0], q_gain), cosine, signed_sine, even).astype(jnp.bfloat16)
    key_rot = rotate(rms_gain(projected[1], k_gain), cosine, signed_sine, even).astype(jnp.bfloat16)
    values = projected[2].astype(jnp.bfloat16)
    own = jnp.stack([key_rot, values])

    to_left = seq_route(spread, lambda x, z, n: (x - 1, z))
    to_right = seq_route(spread, lambda x, z, n: (x + 1, z))
    to_other_z = seq_route(spread, lambda x, z, n: (x, 1 - z))

    def shard_of(x, z):
        return (x % count_x) * 2 + z

    got_z = lax.ppermute(own, "seq", to_other_z)
    got_right = lax.ppermute(own, "seq", to_left)
    got_left = lax.ppermute(own, "seq", to_right)

    softmax_state = (
        jnp.full((heads_here, rows_dev), -jnp.inf, jnp.float32),
        jnp.zeros((heads_here, rows_dev), jnp.float32),
        jnp.zeros((heads_here, rows_dev, head_dim), jnp.float32),
    )
    softmax_state = fold_block(softmax_state, queries, own[0], own[1], shard_pos, text_count)

    z_from_right, far_keys = lax.ppermute((got_z, got_right[0]), "seq", to_left)
    z_from_left, far_values = lax.ppermute((got_z, got_left[1]), "seq", to_right)

    other_z = 1 - my_z
    softmax_state = fold_group(
        softmax_state,
        queries,
        [
            (got_z[0], got_z[1], shard_of(my_x, other_z)),
            (got_right[0], got_right[1], shard_of(my_x + 1, my_z)),
            (got_left[0], got_left[1], shard_of(my_x - 1, my_z)),
        ],
        text_count,
    )

    far_z_keys = lax.ppermute(z_from_right[0], "seq", to_left)
    far_z_values = lax.ppermute(z_from_left[1], "seq", to_right)

    late_state = (
        jnp.full((heads_here, rows_dev), -jnp.inf, jnp.float32),
        jnp.zeros((heads_here, rows_dev), jnp.float32),
        jnp.zeros((heads_here, rows_dev, head_dim), jnp.float32),
    )
    late_state = fold_group(
        late_state,
        queries,
        [
            (far_keys, far_values, shard_of(my_x + 2, my_z)),
            (z_from_right[0], z_from_right[1], shard_of(my_x + 1, other_z)),
            (z_from_left[0], z_from_left[1], shard_of(my_x - 1, other_z)),
        ],
        text_count,
    )
    softmax_state = fold_block(
        softmax_state, queries, far_z_keys, far_z_values, shard_of(my_x + 2, other_z), text_count
    )
    softmax_state = merge_states(softmax_state, late_state)

    row_max, row_sum, weighted = softmax_state
    attended = (weighted / row_sum[:, :, None]).astype(jnp.bfloat16)
    log_sums = row_max + jnp.log(row_sum)
    hold = jnp.minimum(jnp.abs(queries[0, 0, 0]), 0).astype(out_weight.dtype)
    attended_parts = [attended]
    weight_parts = [lax.dynamic_slice_in_dim(out_weight, tp_pos * local_width, local_width, 1)]
    pair_pos = lax.axis_index("pair")
    assert lax.axis_size("pair") == 2
    half = local_width // 2
    fetched = []
    for shift in range(1, tp_count):
        route = [(src, (src + shift) % tp_count) for src in range(tp_count)]
        dest = (tp_pos + shift) % tp_count
        weight_send = lax.dynamic_slice_in_dim(
            out_weight, dest * local_width + pair_pos * half, half, 1
        )
        fetched.append(lax.ppermute(weight_send + hold, "tp", route))
        attended_parts.append(lax.ppermute(attended, "tp", route))
    fetched = jnp.stack(fetched)
    other_half = lax.ppermute(fetched, "pair", [(0, 1), (1, 0)])
    first_half = jnp.where(pair_pos == 0, fetched, other_half)
    second_half = jnp.where(pair_pos == 0, other_half, fetched)
    joined = jnp.concatenate([first_half, second_half], axis=2)
    weight_parts += [joined[index] for index in range(tp_count - 1)]
    all_attended = jnp.stack(attended_parts)
    all_weights = jnp.stack(weight_parts).reshape(tp_count, heads_here, head_dim, local_width)
    update = jnp.einsum(
        "khrd,khdf->rf", all_attended, all_weights, preferred_element_type=jnp.float32
    )
    gate_slice = lax.dynamic_slice_in_dim(layer_terms[2], tp_pos * local_width, local_width, 0)
    new_hidden = (hidden.astype(jnp.float32) + gate_slice * update).astype(jnp.bfloat16)

    final_terms = lax.dynamic_index_in_dim(final_mod, local_seq, 0, keepdims=False)
    final_shift = lax.dynamic_slice_in_dim(final_terms[0], tp_pos * local_width, local_width, 0)
    final_scale = lax.dynamic_slice_in_dim(final_terms[1], tp_pos * local_width, local_width, 0)
    image_rows = new_hidden[:IMG_DEV].astype(jnp.float32)
    weight = final_weight.astype(jnp.float32)
    scale_one = 1.0 + final_scale
    highest = lax.Precision.HIGHEST
    terms = (
        jnp.sum(image_rows, axis=1),
        jnp.sum(image_rows * image_rows, axis=1),
        jnp.dot(image_rows * scale_one, weight, precision=highest),
        jnp.dot(scale_one[None, :], weight, precision=highest),
        jnp.dot(final_shift[None, :], weight, precision=highest),
    )
    row_sums, squares, scaled_proj, scale_proj, shift_proj = tp_sum(terms)
    row_mean = row_sums / model_width
    inv_std = lax.rsqrt(squares / model_width - row_mean * row_mean + 1e-06)
    velocity = (
        inv_std[:, None] * (scaled_proj - row_mean[:, None] * scale_proj) + shift_proj
    )

    half_rows = IMG_DEV // 2
    is_cond = local_seq % 2 == 0
    outgoing = jnp.where(is_cond, velocity[half_rows:], velocity[:half_rows])
    partner_half = swapped(outgoing, "seq", bit_count)
    own_half = jnp.where(is_cond, velocity[:half_rows], velocity[half_rows:])
    cond_vel = jnp.where(is_cond, own_half, partner_half)
    uncond_vel = jnp.where(is_cond, partner_half, own_half)
    guided = uncond_vel + GUIDE * (cond_vel - uncond_vel)
    step_now = step_index[0]
    time_step = sigma_at(step_now + 1) - sigma_at(step_now)
    return (new_hidden, log_sums, latents + time_step * guided)


def solution(mesh):
    return jax.shard_map(
        on_device,
        mesh=mesh,
        in_specs=(
            P(("pair", "seq"), "tp"),
            P(None, ("pair", "seq")),
            P("pair"),
            P(),
            P("pair", None, None),
            P("pair", None, None),
            P(None, None, "tp"),
            P(),
            P(),
            P("tp", None),
            P("tp", None),
            P(("pair", "seq"), None),
        ),
        out_specs=(P(("pair", "seq"), "tp"), P("tp", ("pair", "seq")), P(("pair", "seq"), None)),
        check_vma=False,
    )
```

```python
import jax
import jax.numpy as jnp
from jax import lax
from jax.sharding import PartitionSpec as P

ROPE_T = 16
ROPE_H = 56
ROPE_W = 56
STEPS = 8
IMG_DEV = 512
TXT_DEV = 64


GUIDE = 3.5
SHIFT = 3.0


def swapped(block, axis, bit):
    count = lax.axis_size(axis)
    route = []
    for low in range(count):
        high = low | 1 << bit
        if high != low and high < count:
            route += [(low, high), (high, low)]
    return lax.ppermute(block, axis, route)


def seq_route(spread, move):
    count_x = spread // 2
    route = []
    for group in range(4):
        for shard in range(spread):
            dest_x, dest_z = move(shard // 2, shard % 2, count_x)
            route.append((group * spread + shard, group * spread + (dest_x % count_x) * 2 + dest_z))
    return route


def rope_tables(ids_block):
    angle_parts = []
    for axis_pos, rope_width in ((0, ROPE_T), (1, ROPE_H), (2, ROPE_W)):
        frequencies = 10000.0 ** (-jnp.arange(0, rope_width, 2).astype(jnp.float32) / rope_width)
        angle_parts.append(ids_block[axis_pos].astype(jnp.float32)[:, None] * frequencies[None, :])
    angles = jnp.concatenate(angle_parts, axis=1)
    angles = jnp.repeat(angles, 2, axis=1)
    even = (jnp.arange(angles.shape[1]) % 2 == 0)[None, :]
    sine = jnp.sin(angles)
    return (jnp.cos(angles), jnp.where(even, -sine, sine), even)


def rotate(tensor, cosine, signed_sine, even):
    partner = jnp.where(
        even[None], jnp.roll(tensor, -1, axis=-1), jnp.roll(tensor, 1, axis=-1)
    )
    return tensor * cosine[None] + partner * signed_sine[None]


def rms_gain(tensor, gain_vec):
    return tensor * lax.rsqrt(jnp.mean(tensor * tensor, axis=-1, keepdims=True) + 1e-06) * gain_vec


def modulate(features, shift_vec, scale_vec):
    row_mean = jnp.mean(features, axis=-1, keepdims=True)
    row_var = jnp.mean(features * features, axis=-1, keepdims=True) - row_mean * row_mean
    return (features - row_mean) * lax.rsqrt(row_var + 1e-06) * (1.0 + scale_vec) + shift_vec


def sigma_at(step_now):
    time_now = 1.0 - step_now.astype(jnp.float32) / STEPS
    return SHIFT * time_now / (1.0 + (SHIFT - 1.0) * time_now)


def fold_block(state, queries, key_block, value_block, shard, text_count):
    row_max, row_sum, weighted = state
    rows_dev = key_block.shape[1]
    offset = jnp.arange(rows_dev, dtype=jnp.int32)
    text_index = shard * TXT_DEV + offset - IMG_DEV
    is_live = (offset < IMG_DEV) | (text_index < text_count)
    score_scale = queries.shape[-1] ** (-0.5)
    scores = (
        jnp.einsum("hqd,hkd->hqk", queries, key_block, preferred_element_type=jnp.float32)
        * score_scale
    )
    scores = jnp.where(is_live[None, None, :], scores, -jnp.inf)
    new_max = jnp.maximum(row_max, jnp.max(scores, axis=2))
    exps = jnp.exp(scores - new_max[:, :, None])
    decay = jnp.exp(row_max - new_max)
    row_sum = row_sum * decay + jnp.sum(exps, axis=2)
    weighted = weighted * decay[:, :, None] + jnp.einsum(
        "hqk,hkd->hqd", exps.astype(jnp.bfloat16), value_block, preferred_element_type=jnp.float32
    )
    return (new_max, row_sum, weighted)


def fold_group(state, queries, blocks, text_count):
    rows = blocks[0][0].shape[1]
    offset = jnp.arange(rows, dtype=jnp.int32)
    is_live = jnp.concatenate(
        [(offset < IMG_DEV) | (shard * TXT_DEV + offset - IMG_DEV < text_count) for _, _, shard in blocks]
    )
    key_rows = jnp.concatenate([blk[0] for blk in blocks], axis=1)
    value_rows = jnp.concatenate([blk[1] for blk in blocks], axis=1)
    row_max, row_sum, weighted = state
    score_scale = queries.shape[-1] ** (-0.5)
    scores = (
        jnp.einsum("hqd,hkd->hqk", queries, key_rows, preferred_element_type=jnp.float32)
        * score_scale
    )
    scores = jnp.where(is_live[None, None, :], scores, -jnp.inf)
    new_max = jnp.maximum(row_max, jnp.max(scores, axis=2))
    exps = jnp.exp(scores - new_max[:, :, None])
    decay = jnp.exp(row_max - new_max)
    row_sum = row_sum * decay + jnp.sum(exps, axis=2)
    weighted = weighted * decay[:, :, None] + jnp.einsum(
        "hqk,hkd->hqd", exps.astype(jnp.bfloat16), value_rows, preferred_element_type=jnp.float32
    )
    return (new_max, row_sum, weighted)


def merge_states(first, second):
    max_a, sum_a, acc_a = first
    max_b, sum_b, acc_b = second
    new_max = jnp.maximum(max_a, max_b)
    scale_a = jnp.exp(max_a - new_max)
    scale_b = jnp.exp(max_b - new_max)
    return (
        new_max,
        sum_a * scale_a + sum_b * scale_b,
        acc_a * scale_a[:, :, None] + acc_b * scale_b[:, :, None],
    )


def tp_sum(tree):
    count = lax.axis_size("tp")
    tp_pos = lax.axis_index("tp")
    parts = [tree]
    for shift in range(1, count):
        route = [(src, (src + shift) % count) for src in range(count)]
        parts.append(lax.ppermute(tree, "tp", route))
    stacked = jax.tree.map(lambda *leaves: jnp.stack(leaves), *parts)

    def owner_part(owner):
        return jax.tree.map(
            lambda leaf: lax.dynamic_index_in_dim(leaf, (tp_pos - owner) % count, 0, keepdims=False),
            stacked,
        )

    total = owner_part(0)
    for owner in range(1, count):
        total = jax.tree.map(lambda a, b: a + b, total, owner_part(owner))
    return total


def on_device(
    hidden,
    positions,
    lengths,
    step_index,
    layer_mod,
    final_mod,
    qkv_weight,
    q_gain,
    k_gain,
    out_weight,
    final_weight,
    latents,
):
    spread = lax.axis_size("seq") // 4
    bit_count = spread.bit_length() - 1
    seq_pos = lax.axis_index("seq")
    local_seq = seq_pos // spread
    shard_pos = seq_pos % spread
    count_x = spread // 2
    my_x = shard_pos // 2
    my_z = shard_pos % 2
    tp_pos = lax.axis_index("tp")
    local_width = hidden.shape[1]
    tp_count = lax.axis_size("tp")
    parts = [hidden]
    for shift in range(1, tp_count):
        route = [(src, (src + shift) % tp_count) for src in range(tp_count)]
        parts.append(lax.ppermute(hidden, "tp", route))
    stacked = jnp.stack(parts)
    gathered = jnp.concatenate(
        [
            lax.dynamic_index_in_dim(stacked, (tp_pos - owner) % tp_count, 0, keepdims=False)
            for owner in range(tp_count)
        ],
        axis=1,
    )
    model_width = gathered.shape[1]
    rows_dev = gathered.shape[0]
    layer_terms = lax.dynamic_index_in_dim(layer_mod, local_seq, 0, keepdims=False)
    text_count = lax.dynamic_index_in_dim(lengths, local_seq, 0, keepdims=False)
    modulated = modulate(gathered.astype(jnp.float32), layer_terms[0], layer_terms[1]).astype(
        jnp.bfloat16
    )
    head_dim = q_gain.shape[0]
    head_cols = qkv_weight.shape[2]
    heads_here = head_cols // head_dim
    weight4 = qkv_weight.reshape(model_width, 3, heads_here, head_dim)
    projected = jnp.einsum(
        "rf,fchd->chrd", modulated, weight4, preferred_element_type=jnp.float32
    )
    cosine, signed_sine, even = rope_tables(positions)
    queries = rotate(rms_gain(projected[0], q_gain), cosine, signed_sine, even).astype(jnp.bfloat16)
    key_rot = rotate(rms_gain(projected[1], k_gain), cosine, signed_sine, even).astype(jnp.bfloat16)
    values = projected[2].astype(jnp.bfloat16)
    own = jnp.stack([key_rot, values])

    to_left = seq_route(spread, lambda x, z, n: (x - 1, z))
    to_right = seq_route(spread, lambda x, z, n: (x + 1, z))
    to_other_z = seq_route(spread, lambda x, z, n: (x, 1 - z))

    def shard_of(x, z):
        return (x % count_x) * 2 + z

    got_z = lax.ppermute(own, "seq", to_other_z)
    got_right = lax.ppermute(own, "seq", to_left)
    got_left = lax.ppermute(own, "seq", to_right)

    softmax_state = (
        jnp.full((heads_here, rows_dev), -jnp.inf, jnp.float32),
        jnp.zeros((heads_here, rows_dev), jnp.float32),
        jnp.zeros((heads_here, rows_dev, head_dim), jnp.float32),
    )
    softmax_state = fold_block(softmax_state, queries, own[0], own[1], shard_pos, text_count)

    z_from_right, far_keys = lax.ppermute((got_z, got_right[0]), "seq", to_left)
    z_from_left, far_values = lax.ppermute((got_z, got_left[1]), "seq", to_right)

    other_z = 1 - my_z
    softmax_state = fold_group(
        softmax_state,
        queries,
        [
            (got_z[0], got_z[1], shard_of(my_x, other_z)),
            (got_right[0], got_right[1], shard_of(my_x + 1, my_z)),
            (got_left[0], got_left[1], shard_of(my_x - 1, my_z)),
        ],
        text_count,
    )

    far_z_keys = lax.ppermute(z_from_right[0], "seq", to_left)
    far_z_values = lax.ppermute(z_from_left[1], "seq", to_right)

    late_state = (
        jnp.full((heads_here, rows_dev), -jnp.inf, jnp.float32),
        jnp.zeros((heads_here, rows_dev), jnp.float32),
        jnp.zeros((heads_here, rows_dev, head_dim), jnp.float32),
    )
    late_state = fold_group(
        late_state,
        queries,
        [
            (far_keys, far_values, shard_of(my_x + 2, my_z)),
            (z_from_right[0], z_from_right[1], shard_of(my_x + 1, other_z)),
            (z_from_left[0], z_from_left[1], shard_of(my_x - 1, other_z)),
        ],
        text_count,
    )
    softmax_state = fold_block(
        softmax_state, queries, far_z_keys, far_z_values, shard_of(my_x + 2, other_z), text_count
    )
    softmax_state = merge_states(softmax_state, late_state)

    row_max, row_sum, weighted = softmax_state
    attended = (weighted / row_sum[:, :, None]).astype(jnp.bfloat16)
    log_sums = row_max + jnp.log(row_sum)
    hold = jnp.minimum(jnp.abs(queries[0, 0, 0]), 0).astype(out_weight.dtype)
    attended_parts = [attended]
    weight_parts = [lax.dynamic_slice_in_dim(out_weight, tp_pos * local_width, local_width, 1)]
    for shift in range(1, tp_count):
        route = [(src, (src + shift) % tp_count) for src in range(tp_count)]
        dest = (tp_pos + shift) % tp_count
        weight_send = lax.dynamic_slice_in_dim(out_weight, dest * local_width, local_width, 1)
        weight_parts.append(lax.ppermute(weight_send + hold, "tp", route))
        attended_parts.append(lax.ppermute(attended, "tp", route))
    all_attended = jnp.stack(attended_parts)
    all_weights = jnp.stack(weight_parts).reshape(tp_count, heads_here, head_dim, local_width)
    update = jnp.einsum(
        "khrd,khdf->rf", all_attended, all_weights, preferred_element_type=jnp.float32
    )
    gate_slice = lax.dynamic_slice_in_dim(layer_terms[2], tp_pos * local_width, local_width, 0)
    new_hidden = (hidden.astype(jnp.float32) + gate_slice * update).astype(jnp.bfloat16)

    final_terms = lax.dynamic_index_in_dim(final_mod, local_seq, 0, keepdims=False)
    final_shift = lax.dynamic_slice_in_dim(final_terms[0], tp_pos * local_width, local_width, 0)
    final_scale = lax.dynamic_slice_in_dim(final_terms[1], tp_pos * local_width, local_width, 0)
    image_rows = new_hidden[:IMG_DEV].astype(jnp.float32)
    weight = final_weight.astype(jnp.float32)
    scale_one = 1.0 + final_scale
    highest = lax.Precision.HIGHEST
    terms = (
        jnp.sum(image_rows, axis=1),
        jnp.sum(image_rows * image_rows, axis=1),
        jnp.dot(image_rows * scale_one, weight, precision=highest),
        jnp.dot(scale_one[None, :], weight, precision=highest),
        jnp.dot(final_shift[None, :], weight, precision=highest),
    )
    row_sums, squares, scaled_proj, scale_proj, shift_proj = tp_sum(terms)
    row_mean = row_sums / model_width
    inv_std = lax.rsqrt(squares / model_width - row_mean * row_mean + 1e-06)
    velocity = (
        inv_std[:, None] * (scaled_proj - row_mean[:, None] * scale_proj) + shift_proj
    )

    half_rows = IMG_DEV // 2
    is_cond = local_seq % 2 == 0
    outgoing = jnp.where(is_cond, velocity[half_rows:], velocity[:half_rows])
    partner_half = swapped(outgoing, "seq", bit_count)
    own_half = jnp.where(is_cond, velocity[:half_rows], velocity[half_rows:])
    cond_vel = jnp.where(is_cond, own_half, partner_half)
    uncond_vel = jnp.where(is_cond, partner_half, own_half)
    guided = uncond_vel + GUIDE * (cond_vel - uncond_vel)
    step_now = step_index[0]
    time_step = sigma_at(step_now + 1) - sigma_at(step_now)
    return (new_hidden, log_sums, latents + time_step * guided)


def solution(mesh):
    return jax.shard_map(
        on_device,
        mesh=mesh,
        in_specs=(
            P(("pair", "seq"), "tp"),
            P(None, ("pair", "seq")),
            P("pair"),
            P(),
            P("pair", None, None),
            P("pair", None, None),
            P(None, None, "tp"),
            P(),
            P(),
            P("tp", None),
            P("tp", None),
            P(("pair", "seq"), None),
        ),
        out_specs=(P(("pair", "seq"), "tp"), P("tp", ("pair", "seq")), P(("pair", "seq"), None)),
        check_vma=False,
    )
```

```python
import jax
import jax.numpy as jnp
from jax import lax
from jax.sharding import PartitionSpec as P

ROPE_T = 16
ROPE_H = 56
ROPE_W = 56
STEPS = 8
IMG_DEV = 512
TXT_DEV = 64


GUIDE = 3.5
SHIFT = 3.0


def swapped(block, axis, bit):
    count = lax.axis_size(axis)
    route = []
    for low in range(count):
        high = low | 1 << bit
        if high != low and high < count:
            route += [(low, high), (high, low)]
    return lax.ppermute(block, axis, route)


def seq_route(spread, move):
    count_x = spread // 2
    route = []
    for group in range(4):
        for shard in range(spread):
            dest_x, dest_z = move(shard // 2, shard % 2, count_x)
            route.append((group * spread + shard, group * spread + (dest_x % count_x) * 2 + dest_z))
    return route


def rope_tables(ids_block):
    angle_parts = []
    for axis_pos, rope_width in ((0, ROPE_T), (1, ROPE_H), (2, ROPE_W)):
        frequencies = 10000.0 ** (-jnp.arange(0, rope_width, 2).astype(jnp.float32) / rope_width)
        angle_parts.append(ids_block[axis_pos].astype(jnp.float32)[:, None] * frequencies[None, :])
    angles = jnp.concatenate(angle_parts, axis=1)
    angles = jnp.repeat(angles, 2, axis=1)
    even = (jnp.arange(angles.shape[1]) % 2 == 0)[None, :]
    sine = jnp.sin(angles)
    return (jnp.cos(angles), jnp.where(even, -sine, sine), even)


def rotate(tensor, cosine, signed_sine, even):
    partner = jnp.where(
        even[None], jnp.roll(tensor, -1, axis=-1), jnp.roll(tensor, 1, axis=-1)
    )
    return tensor * cosine[None] + partner * signed_sine[None]


def rms_gain(tensor, gain_vec):
    return tensor * lax.rsqrt(jnp.mean(tensor * tensor, axis=-1, keepdims=True) + 1e-06) * gain_vec


def modulate(features, shift_vec, scale_vec):
    row_mean = jnp.mean(features, axis=-1, keepdims=True)
    row_var = jnp.mean(features * features, axis=-1, keepdims=True) - row_mean * row_mean
    return (features - row_mean) * lax.rsqrt(row_var + 1e-06) * (1.0 + scale_vec) + shift_vec


def sigma_at(step_now):
    time_now = 1.0 - step_now.astype(jnp.float32) / STEPS
    return SHIFT * time_now / (1.0 + (SHIFT - 1.0) * time_now)


def fold_block(state, queries, key_block, value_block, shard, text_count):
    row_max, row_sum, weighted = state
    rows_dev = key_block.shape[1]
    offset = jnp.arange(rows_dev, dtype=jnp.int32)
    text_index = shard * TXT_DEV + offset - IMG_DEV
    is_live = (offset < IMG_DEV) | (text_index < text_count)
    score_scale = queries.shape[-1] ** (-0.5)
    scores = (
        jnp.einsum("hqd,hkd->hqk", queries, key_block, preferred_element_type=jnp.float32)
        * score_scale
    )
    scores = jnp.where(is_live[None, None, :], scores, -jnp.inf)
    new_max = jnp.maximum(row_max, jnp.max(scores, axis=2))
    exps = jnp.exp(scores - new_max[:, :, None])
    decay = jnp.exp(row_max - new_max)
    row_sum = row_sum * decay + jnp.sum(exps, axis=2)
    weighted = weighted * decay[:, :, None] + jnp.einsum(
        "hqk,hkd->hqd", exps.astype(jnp.bfloat16), value_block, preferred_element_type=jnp.float32
    )
    return (new_max, row_sum, weighted)


def fold_group(state, queries, blocks, text_count):
    rows = blocks[0][0].shape[1]
    offset = jnp.arange(rows, dtype=jnp.int32)
    is_live = jnp.concatenate(
        [(offset < IMG_DEV) | (shard * TXT_DEV + offset - IMG_DEV < text_count) for _, _, shard in blocks]
    )
    key_rows = jnp.concatenate([blk[0] for blk in blocks], axis=1)
    value_rows = jnp.concatenate([blk[1] for blk in blocks], axis=1)
    row_max, row_sum, weighted = state
    score_scale = queries.shape[-1] ** (-0.5)
    scores = (
        jnp.einsum("hqd,hkd->hqk", queries, key_rows, preferred_element_type=jnp.float32)
        * score_scale
    )
    scores = jnp.where(is_live[None, None, :], scores, -jnp.inf)
    new_max = jnp.maximum(row_max, jnp.max(scores, axis=2))
    exps = jnp.exp(scores - new_max[:, :, None])
    decay = jnp.exp(row_max - new_max)
    row_sum = row_sum * decay + jnp.sum(exps, axis=2)
    weighted = weighted * decay[:, :, None] + jnp.einsum(
        "hqk,hkd->hqd", exps.astype(jnp.bfloat16), value_rows, preferred_element_type=jnp.float32
    )
    return (new_max, row_sum, weighted)


def merge_states(first, second):
    max_a, sum_a, acc_a = first
    max_b, sum_b, acc_b = second
    new_max = jnp.maximum(max_a, max_b)
    scale_a = jnp.exp(max_a - new_max)
    scale_b = jnp.exp(max_b - new_max)
    return (
        new_max,
        sum_a * scale_a + sum_b * scale_b,
        acc_a * scale_a[:, :, None] + acc_b * scale_b[:, :, None],
    )


def tp_sum(tree):
    count = lax.axis_size("tp")
    bit = 0
    while 1 << bit < count:
        far = swapped(tree, "tp", bit)
        tree = jax.tree.map(lambda a, b: a + b, tree, far)
        bit += 1
    return tree


def on_device(
    hidden,
    positions,
    lengths,
    step_index,
    layer_mod,
    final_mod,
    qkv_weight,
    q_gain,
    k_gain,
    out_weight,
    final_weight,
    latents,
):
    spread = lax.axis_size("seq") // 4
    bit_count = spread.bit_length() - 1
    seq_pos = lax.axis_index("seq")
    local_seq = seq_pos // spread
    shard_pos = seq_pos % spread
    count_x = spread // 2
    my_x = shard_pos // 2
    my_z = shard_pos % 2
    tp_pos = lax.axis_index("tp")
    local_width = hidden.shape[1]
    tp_count = lax.axis_size("tp")
    parts = [hidden]
    for shift in range(1, tp_count):
        route = [(src, (src + shift) % tp_count) for src in range(tp_count)]
        parts.append(lax.ppermute(hidden, "tp", route))
    stacked = jnp.stack(parts)
    gathered = jnp.concatenate(
        [
            lax.dynamic_index_in_dim(stacked, (tp_pos - owner) % tp_count, 0, keepdims=False)
            for owner in range(tp_count)
        ],
        axis=1,
    )
    model_width = gathered.shape[1]
    rows_dev = gathered.shape[0]
    layer_terms = lax.dynamic_index_in_dim(layer_mod, local_seq, 0, keepdims=False)
    text_count = lax.dynamic_index_in_dim(lengths, local_seq, 0, keepdims=False)
    modulated = modulate(gathered.astype(jnp.float32), layer_terms[0], layer_terms[1]).astype(
        jnp.bfloat16
    )
    head_dim = q_gain.shape[0]
    head_cols = qkv_weight.shape[2]
    heads_here = head_cols // head_dim
    weight4 = qkv_weight.reshape(model_width, 3, heads_here, head_dim)
    projected = jnp.einsum(
        "rf,fchd->chrd", modulated, weight4, preferred_element_type=jnp.float32
    )
    cosine, signed_sine, even = rope_tables(positions)
    queries = rotate(rms_gain(projected[0], q_gain), cosine, signed_sine, even).astype(jnp.bfloat16)
    key_rot = rotate(rms_gain(projected[1], k_gain), cosine, signed_sine, even).astype(jnp.bfloat16)
    values = projected[2].astype(jnp.bfloat16)
    own = jnp.stack([key_rot, values])

    to_left = seq_route(spread, lambda x, z, n: (x - 1, z))
    to_right = seq_route(spread, lambda x, z, n: (x + 1, z))
    to_other_z = seq_route(spread, lambda x, z, n: (x, 1 - z))

    def shard_of(x, z):
        return (x % count_x) * 2 + z

    got_z = lax.ppermute(own, "seq", to_other_z)
    got_right = lax.ppermute(own, "seq", to_left)
    got_left = lax.ppermute(own, "seq", to_right)

    softmax_state = (
        jnp.full((heads_here, rows_dev), -jnp.inf, jnp.float32),
        jnp.zeros((heads_here, rows_dev), jnp.float32),
        jnp.zeros((heads_here, rows_dev, head_dim), jnp.float32),
    )
    softmax_state = fold_block(softmax_state, queries, own[0], own[1], shard_pos, text_count)

    z_from_right, far_keys = lax.ppermute((got_z, got_right[0]), "seq", to_left)
    z_from_left, far_values = lax.ppermute((got_z, got_left[1]), "seq", to_right)

    other_z = 1 - my_z
    softmax_state = fold_group(
        softmax_state,
        queries,
        [
            (got_z[0], got_z[1], shard_of(my_x, other_z)),
            (got_right[0], got_right[1], shard_of(my_x + 1, my_z)),
            (got_left[0], got_left[1], shard_of(my_x - 1, my_z)),
        ],
        text_count,
    )

    far_z_keys = lax.ppermute(z_from_right[0], "seq", to_left)
    far_z_values = lax.ppermute(z_from_left[1], "seq", to_right)

    late_state = (
        jnp.full((heads_here, rows_dev), -jnp.inf, jnp.float32),
        jnp.zeros((heads_here, rows_dev), jnp.float32),
        jnp.zeros((heads_here, rows_dev, head_dim), jnp.float32),
    )
    late_state = fold_group(
        late_state,
        queries,
        [
            (far_keys, far_values, shard_of(my_x + 2, my_z)),
            (z_from_right[0], z_from_right[1], shard_of(my_x + 1, other_z)),
            (z_from_left[0], z_from_left[1], shard_of(my_x - 1, other_z)),
        ],
        text_count,
    )
    softmax_state = fold_block(
        softmax_state, queries, far_z_keys, far_z_values, shard_of(my_x + 2, other_z), text_count
    )
    softmax_state = merge_states(softmax_state, late_state)

    row_max, row_sum, weighted = softmax_state
    attended = (weighted / row_sum[:, :, None]).astype(jnp.bfloat16)
    log_sums = row_max + jnp.log(row_sum)
    hold = jnp.minimum(jnp.abs(queries[0, 0, 0]), 0).astype(out_weight.dtype)
    attended_parts = [attended]
    for shift in range(1, tp_count):
        route = [(src, (src + shift) % tp_count) for src in range(tp_count)]
        attended_parts.append(lax.ppermute(attended, "tp", route))
    attended_stack = jnp.stack(attended_parts)
    all_attended = jnp.stack(
        [
            lax.dynamic_index_in_dim(attended_stack, (tp_pos - owner) % tp_count, 0, keepdims=False)
            for owner in range(tp_count)
        ]
    )
    all_weights = lax.all_to_all(out_weight + hold, "tp", 1, 0, tiled=True).reshape(
        tp_count, heads_here, head_dim, local_width
    )
    update = jnp.einsum(
        "khrd,khdf->rf", all_attended, all_weights, preferred_element_type=jnp.float32
    )
    gate_slice = lax.dynamic_slice_in_dim(layer_terms[2], tp_pos * local_width, local_width, 0)
    new_hidden = (hidden.astype(jnp.float32) + gate_slice * update).astype(jnp.bfloat16)

    final_terms = lax.dynamic_index_in_dim(final_mod, local_seq, 0, keepdims=False)
    final_shift = lax.dynamic_slice_in_dim(final_terms[0], tp_pos * local_width, local_width, 0)
    final_scale = lax.dynamic_slice_in_dim(final_terms[1], tp_pos * local_width, local_width, 0)
    image_rows = new_hidden[:IMG_DEV].astype(jnp.float32)
    weight = final_weight.astype(jnp.float32)
    scale_one = 1.0 + final_scale
    highest = lax.Precision.HIGHEST
    terms = (
        jnp.sum(image_rows, axis=1),
        jnp.sum(image_rows * image_rows, axis=1),
        jnp.dot(image_rows * scale_one, weight, precision=highest),
        jnp.dot(scale_one[None, :], weight, precision=highest),
        jnp.dot(final_shift[None, :], weight, precision=highest),
    )
    row_sums, squares, scaled_proj, scale_proj, shift_proj = tp_sum(terms)
    row_mean = row_sums / model_width
    inv_std = lax.rsqrt(squares / model_width - row_mean * row_mean + 1e-06)
    velocity = (
        inv_std[:, None] * (scaled_proj - row_mean[:, None] * scale_proj) + shift_proj
    )

    half_rows = IMG_DEV // 2
    is_cond = local_seq % 2 == 0
    outgoing = jnp.where(is_cond, velocity[half_rows:], velocity[:half_rows])
    partner_half = swapped(outgoing, "seq", bit_count)
    own_half = jnp.where(is_cond, velocity[:half_rows], velocity[half_rows:])
    cond_vel = jnp.where(is_cond, own_half, partner_half)
    uncond_vel = jnp.where(is_cond, partner_half, own_half)
    guided = uncond_vel + GUIDE * (cond_vel - uncond_vel)
    step_now = step_index[0]
    time_step = sigma_at(step_now + 1) - sigma_at(step_now)
    return (new_hidden, log_sums, latents + time_step * guided)


def solution(mesh):
    return jax.shard_map(
        on_device,
        mesh=mesh,
        in_specs=(
            P(("pair", "seq"), "tp"),
            P(None, ("pair", "seq")),
            P("pair"),
            P(),
            P("pair", None, None),
            P("pair", None, None),
            P(None, None, "tp"),
            P(),
            P(),
            P("tp", None),
            P("tp", None),
            P(("pair", "seq"), None),
        ),
        out_specs=(P(("pair", "seq"), "tp"), P("tp", ("pair", "seq")), P(("pair", "seq"), None)),
        check_vma=False,
    )
```

```python
import jax
import jax.numpy as jnp
from jax import lax
from jax.sharding import PartitionSpec as P

ROPE_T = 16
ROPE_H = 56
ROPE_W = 56
STEPS = 8
IMG_DEV = 512
TXT_DEV = 64


GUIDE = 3.5
SHIFT = 3.0


def swapped(block, axis, bit):
    count = lax.axis_size(axis)
    route = []
    for low in range(count):
        high = low | 1 << bit
        if high != low and high < count:
            route += [(low, high), (high, low)]
    return lax.ppermute(block, axis, route)


def seq_route(spread, move):
    count_x = spread // 2
    route = []
    for group in range(4):
        for shard in range(spread):
            dest_x, dest_z = move(shard // 2, shard % 2, count_x)
            route.append((group * spread + shard, group * spread + (dest_x % count_x) * 2 + dest_z))
    return route


def rope_tables(ids_block):
    angle_parts = []
    for axis_pos, rope_width in ((0, ROPE_T), (1, ROPE_H), (2, ROPE_W)):
        frequencies = 10000.0 ** (-jnp.arange(0, rope_width, 2).astype(jnp.float32) / rope_width)
        angle_parts.append(ids_block[axis_pos].astype(jnp.float32)[:, None] * frequencies[None, :])
    angles = jnp.concatenate(angle_parts, axis=1)
    angles = jnp.repeat(angles, 2, axis=1)
    even = (jnp.arange(angles.shape[1]) % 2 == 0)[None, :]
    sine = jnp.sin(angles)
    return (jnp.cos(angles), jnp.where(even, -sine, sine), even)


def rotate(tensor, cosine, signed_sine, even):
    partner = jnp.where(
        even[None], jnp.roll(tensor, -1, axis=-1), jnp.roll(tensor, 1, axis=-1)
    )
    return tensor * cosine[None] + partner * signed_sine[None]


def rms_gain(tensor, gain_vec):
    return tensor * lax.rsqrt(jnp.mean(tensor * tensor, axis=-1, keepdims=True) + 1e-06) * gain_vec


def modulate(features, shift_vec, scale_vec):
    row_mean = jnp.mean(features, axis=-1, keepdims=True)
    row_var = jnp.mean(features * features, axis=-1, keepdims=True) - row_mean * row_mean
    return (features - row_mean) * lax.rsqrt(row_var + 1e-06) * (1.0 + scale_vec) + shift_vec


def sigma_at(step_now):
    time_now = 1.0 - step_now.astype(jnp.float32) / STEPS
    return SHIFT * time_now / (1.0 + (SHIFT - 1.0) * time_now)


def fold_block(state, queries, key_block, value_block, shard, text_count):
    row_max, row_sum, weighted = state
    rows_dev = key_block.shape[1]
    offset = jnp.arange(rows_dev, dtype=jnp.int32)
    text_index = shard * TXT_DEV + offset - IMG_DEV
    is_live = (offset < IMG_DEV) | (text_index < text_count)
    score_scale = queries.shape[-1] ** (-0.5)
    scores = (
        jnp.einsum("hqd,hkd->hqk", queries, key_block, preferred_element_type=jnp.float32)
        * score_scale
    )
    scores = jnp.where(is_live[None, None, :], scores, -jnp.inf)
    new_max = jnp.maximum(row_max, jnp.max(scores, axis=2))
    exps = jnp.exp(scores - new_max[:, :, None])
    decay = jnp.exp(row_max - new_max)
    row_sum = row_sum * decay + jnp.sum(exps, axis=2)
    weighted = weighted * decay[:, :, None] + jnp.einsum(
        "hqk,hkd->hqd", exps.astype(jnp.bfloat16), value_block, preferred_element_type=jnp.float32
    )
    return (new_max, row_sum, weighted)


def fold_group(state, queries, blocks, text_count):
    rows = blocks[0][0].shape[1]
    offset = jnp.arange(rows, dtype=jnp.int32)
    is_live = jnp.concatenate(
        [(offset < IMG_DEV) | (shard * TXT_DEV + offset - IMG_DEV < text_count) for _, _, shard in blocks]
    )
    key_rows = jnp.concatenate([blk[0] for blk in blocks], axis=1)
    value_rows = jnp.concatenate([blk[1] for blk in blocks], axis=1)
    row_max, row_sum, weighted = state
    score_scale = queries.shape[-1] ** (-0.5)
    scores = (
        jnp.einsum("hqd,hkd->hqk", queries, key_rows, preferred_element_type=jnp.float32)
        * score_scale
    )
    scores = jnp.where(is_live[None, None, :], scores, -jnp.inf)
    new_max = jnp.maximum(row_max, jnp.max(scores, axis=2))
    exps = jnp.exp(scores - new_max[:, :, None])
    decay = jnp.exp(row_max - new_max)
    row_sum = row_sum * decay + jnp.sum(exps, axis=2)
    weighted = weighted * decay[:, :, None] + jnp.einsum(
        "hqk,hkd->hqd", exps.astype(jnp.bfloat16), value_rows, preferred_element_type=jnp.float32
    )
    return (new_max, row_sum, weighted)


def merge_states(first, second):
    max_a, sum_a, acc_a = first
    max_b, sum_b, acc_b = second
    new_max = jnp.maximum(max_a, max_b)
    scale_a = jnp.exp(max_a - new_max)
    scale_b = jnp.exp(max_b - new_max)
    return (
        new_max,
        sum_a * scale_a + sum_b * scale_b,
        acc_a * scale_a[:, :, None] + acc_b * scale_b[:, :, None],
    )


def tp_sum(tree):
    count = lax.axis_size("tp")
    bit = 0
    while 1 << bit < count:
        far = swapped(tree, "tp", bit)
        tree = jax.tree.map(lambda a, b: a + b, tree, far)
        bit += 1
    return tree


def on_device(
    hidden,
    positions,
    lengths,
    step_index,
    layer_mod,
    final_mod,
    qkv_weight,
    q_gain,
    k_gain,
    out_weight,
    final_weight,
    latents,
):
    spread = lax.axis_size("seq") // 4
    bit_count = spread.bit_length() - 1
    seq_pos = lax.axis_index("seq")
    local_seq = seq_pos // spread
    shard_pos = seq_pos % spread
    count_x = spread // 2
    my_x = shard_pos // 2
    my_z = shard_pos % 2
    tp_pos = lax.axis_index("tp")
    local_width = hidden.shape[1]
    tp_count = lax.axis_size("tp")
    parts = [hidden]
    for shift in range(1, tp_count):
        route = [(src, (src + shift) % tp_count) for src in range(tp_count)]
        parts.append(lax.ppermute(hidden, "tp", route))
    stacked = jnp.stack(parts)
    gathered = jnp.concatenate(
        [
            lax.dynamic_index_in_dim(stacked, (tp_pos - owner) % tp_count, 0, keepdims=False)
            for owner in range(tp_count)
        ],
        axis=1,
    )
    model_width = gathered.shape[1]
    rows_dev = gathered.shape[0]
    layer_terms = lax.dynamic_index_in_dim(layer_mod, local_seq, 0, keepdims=False)
    text_count = lax.dynamic_index_in_dim(lengths, local_seq, 0, keepdims=False)
    modulated = modulate(gathered.astype(jnp.float32), layer_terms[0], layer_terms[1]).astype(
        jnp.bfloat16
    )
    head_dim = q_gain.shape[0]
    head_cols = qkv_weight.shape[2]
    heads_here = head_cols // head_dim
    weight4 = qkv_weight.reshape(model_width, 3, heads_here, head_dim)
    projected = jnp.einsum(
        "rf,fchd->chrd", modulated, weight4, preferred_element_type=jnp.float32
    )
    cosine, signed_sine, even = rope_tables(positions)
    queries = rotate(rms_gain(projected[0], q_gain), cosine, signed_sine, even).astype(jnp.bfloat16)
    key_rot = rotate(rms_gain(projected[1], k_gain), cosine, signed_sine, even).astype(jnp.bfloat16)
    values = projected[2].astype(jnp.bfloat16)
    own = jnp.stack([key_rot, values])

    to_left = seq_route(spread, lambda x, z, n: (x - 1, z))
    to_right = seq_route(spread, lambda x, z, n: (x + 1, z))
    to_other_z = seq_route(spread, lambda x, z, n: (x, 1 - z))

    def shard_of(x, z):
        return (x % count_x) * 2 + z

    got_z = lax.ppermute(own, "seq", to_other_z)
    got_right = lax.ppermute(own, "seq", to_left)
    got_left = lax.ppermute(own, "seq", to_right)

    softmax_state = (
        jnp.full((heads_here, rows_dev), -jnp.inf, jnp.float32),
        jnp.zeros((heads_here, rows_dev), jnp.float32),
        jnp.zeros((heads_here, rows_dev, head_dim), jnp.float32),
    )
    softmax_state = fold_block(softmax_state, queries, own[0], own[1], shard_pos, text_count)

    z_from_right, far_keys = lax.ppermute((got_z, got_right[0]), "seq", to_left)
    z_from_left, far_values = lax.ppermute((got_z, got_left[1]), "seq", to_right)

    other_z = 1 - my_z
    softmax_state = fold_group(
        softmax_state,
        queries,
        [
            (got_z[0], got_z[1], shard_of(my_x, other_z)),
            (got_right[0], got_right[1], shard_of(my_x + 1, my_z)),
            (got_left[0], got_left[1], shard_of(my_x - 1, my_z)),
        ],
        text_count,
    )

    far_z_keys = lax.ppermute(z_from_right[0], "seq", to_left)
    far_z_values = lax.ppermute(z_from_left[1], "seq", to_right)

    late_state = (
        jnp.full((heads_here, rows_dev), -jnp.inf, jnp.float32),
        jnp.zeros((heads_here, rows_dev), jnp.float32),
        jnp.zeros((heads_here, rows_dev, head_dim), jnp.float32),
    )
    late_state = fold_group(
        late_state,
        queries,
        [
            (far_keys, far_values, shard_of(my_x + 2, my_z)),
            (z_from_right[0], z_from_right[1], shard_of(my_x + 1, other_z)),
            (z_from_left[0], z_from_left[1], shard_of(my_x - 1, other_z)),
        ],
        text_count,
    )
    softmax_state = fold_block(
        softmax_state, queries, far_z_keys, far_z_values, shard_of(my_x + 2, other_z), text_count
    )
    softmax_state = merge_states(softmax_state, late_state)

    row_max, row_sum, weighted = softmax_state
    attended = (weighted / row_sum[:, :, None]).astype(jnp.bfloat16)
    log_sums = row_max + jnp.log(row_sum)
    hold = jnp.minimum(jnp.abs(far_z_keys[0, 0, 0]), 0).astype(out_weight.dtype)
    attended_parts = [attended]
    weight_parts = [lax.dynamic_slice_in_dim(out_weight, tp_pos * local_width, local_width, 1)]
    for shift in range(1, tp_count):
        route = [(src, (src + shift) % tp_count) for src in range(tp_count)]
        dest = (tp_pos + shift) % tp_count
        weight_send = lax.dynamic_slice_in_dim(out_weight, dest * local_width, local_width, 1)
        weight_parts.append(lax.ppermute(weight_send + hold, "tp", route))
        attended_parts.append(lax.ppermute(attended, "tp", route))
    all_attended = jnp.stack(attended_parts)
    all_weights = jnp.stack(weight_parts).reshape(tp_count, heads_here, head_dim, local_width)
    update = jnp.einsum(
        "khrd,khdf->rf", all_attended, all_weights, preferred_element_type=jnp.float32
    )
    gate_slice = lax.dynamic_slice_in_dim(layer_terms[2], tp_pos * local_width, local_width, 0)
    new_hidden = (hidden.astype(jnp.float32) + gate_slice * update).astype(jnp.bfloat16)

    final_terms = lax.dynamic_index_in_dim(final_mod, local_seq, 0, keepdims=False)
    final_shift = lax.dynamic_slice_in_dim(final_terms[0], tp_pos * local_width, local_width, 0)
    final_scale = lax.dynamic_slice_in_dim(final_terms[1], tp_pos * local_width, local_width, 0)
    image_rows = new_hidden[:IMG_DEV].astype(jnp.float32)
    weight = final_weight.astype(jnp.float32)
    scale_one = 1.0 + final_scale
    highest = lax.Precision.HIGHEST
    terms = (
        jnp.sum(image_rows, axis=1),
        jnp.sum(image_rows * image_rows, axis=1),
        jnp.dot(image_rows * scale_one, weight, precision=highest),
        jnp.dot(scale_one[None, :], weight, precision=highest),
        jnp.dot(final_shift[None, :], weight, precision=highest),
    )
    row_sums, squares, scaled_proj, scale_proj, shift_proj = tp_sum(terms)
    row_mean = row_sums / model_width
    inv_std = lax.rsqrt(squares / model_width - row_mean * row_mean + 1e-06)
    velocity = (
        inv_std[:, None] * (scaled_proj - row_mean[:, None] * scale_proj) + shift_proj
    )

    half_rows = IMG_DEV // 2
    is_cond = local_seq % 2 == 0
    outgoing = jnp.where(is_cond, velocity[half_rows:], velocity[:half_rows])
    partner_half = swapped(outgoing, "seq", bit_count)
    own_half = jnp.where(is_cond, velocity[:half_rows], velocity[half_rows:])
    cond_vel = jnp.where(is_cond, own_half, partner_half)
    uncond_vel = jnp.where(is_cond, partner_half, own_half)
    guided = uncond_vel + GUIDE * (cond_vel - uncond_vel)
    step_now = step_index[0]
    time_step = sigma_at(step_now + 1) - sigma_at(step_now)
    return (new_hidden, log_sums, latents + time_step * guided)


def solution(mesh):
    return jax.shard_map(
        on_device,
        mesh=mesh,
        in_specs=(
            P(("pair", "seq"), "tp"),
            P(None, ("pair", "seq")),
            P("pair"),
            P(),
            P("pair", None, None),
            P("pair", None, None),
            P(None, None, "tp"),
            P(),
            P(),
            P("tp", None),
            P("tp", None),
            P(("pair", "seq"), None),
        ),
        out_specs=(P(("pair", "seq"), "tp"), P("tp", ("pair", "seq")), P(("pair", "seq"), None)),
        check_vma=False,
    )
```

```python
import jax
import jax.numpy as jnp
from jax import lax
from jax.sharding import PartitionSpec as P

ROPE_T = 16
ROPE_H = 56
ROPE_W = 56
STEPS = 8
IMG_DEV = 512
TXT_DEV = 64


GUIDE = 3.5
SHIFT = 3.0


def swapped(block, axis, bit):
    count = lax.axis_size(axis)
    route = []
    for low in range(count):
        high = low | 1 << bit
        if high != low and high < count:
            route += [(low, high), (high, low)]
    return lax.ppermute(block, axis, route)


def seq_route(spread, move):
    count_x = spread // 2
    route = []
    for group in range(4):
        for shard in range(spread):
            dest_x, dest_z = move(shard // 2, shard % 2, count_x)
            route.append((group * spread + shard, group * spread + (dest_x % count_x) * 2 + dest_z))
    return route


def rope_tables(ids_block):
    angle_parts = []
    for axis_pos, rope_width in ((0, ROPE_T), (1, ROPE_H), (2, ROPE_W)):
        frequencies = 10000.0 ** (-jnp.arange(0, rope_width, 2).astype(jnp.float32) / rope_width)
        angle_parts.append(ids_block[axis_pos].astype(jnp.float32)[:, None] * frequencies[None, :])
    angles = jnp.concatenate(angle_parts, axis=1)
    angles = jnp.repeat(angles, 2, axis=1)
    even = (jnp.arange(angles.shape[1]) % 2 == 0)[None, :]
    sine = jnp.sin(angles)
    return (jnp.cos(angles), jnp.where(even, -sine, sine), even)


def rotate(tensor, cosine, signed_sine, even):
    partner = jnp.where(
        even[None], jnp.roll(tensor, -1, axis=-1), jnp.roll(tensor, 1, axis=-1)
    )
    return tensor * cosine[None] + partner * signed_sine[None]


def rms_gain(tensor, gain_vec):
    return tensor * lax.rsqrt(jnp.mean(tensor * tensor, axis=-1, keepdims=True) + 1e-06) * gain_vec


def modulate(features, shift_vec, scale_vec):
    row_mean = jnp.mean(features, axis=-1, keepdims=True)
    row_var = jnp.mean(features * features, axis=-1, keepdims=True) - row_mean * row_mean
    return (features - row_mean) * lax.rsqrt(row_var + 1e-06) * (1.0 + scale_vec) + shift_vec


def sigma_at(step_now):
    time_now = 1.0 - step_now.astype(jnp.float32) / STEPS
    return SHIFT * time_now / (1.0 + (SHIFT - 1.0) * time_now)


def fold_block(state, queries, key_block, value_block, shard, text_count):
    row_max, row_sum, weighted = state
    rows_dev = key_block.shape[1]
    offset = jnp.arange(rows_dev, dtype=jnp.int32)
    text_index = shard * TXT_DEV + offset - IMG_DEV
    is_live = (offset < IMG_DEV) | (text_index < text_count)
    score_scale = queries.shape[-1] ** (-0.5)
    scores = (
        jnp.einsum("hqd,hkd->hqk", queries, key_block, preferred_element_type=jnp.float32)
        * score_scale
    )
    scores = jnp.where(is_live[None, None, :], scores, -jnp.inf)
    new_max = jnp.maximum(row_max, jnp.max(scores, axis=2))
    exps = jnp.exp(scores - new_max[:, :, None])
    decay = jnp.exp(row_max - new_max)
    row_sum = row_sum * decay + jnp.sum(exps, axis=2)
    weighted = weighted * decay[:, :, None] + jnp.einsum(
        "hqk,hkd->hqd", exps.astype(jnp.bfloat16), value_block, preferred_element_type=jnp.float32
    )
    return (new_max, row_sum, weighted)


def fold_group(state, queries, blocks, text_count):
    rows = blocks[0][0].shape[1]
    offset = jnp.arange(rows, dtype=jnp.int32)
    is_live = jnp.concatenate(
        [(offset < IMG_DEV) | (shard * TXT_DEV + offset - IMG_DEV < text_count) for _, _, shard in blocks]
    )
    key_rows = jnp.concatenate([blk[0] for blk in blocks], axis=1)
    value_rows = jnp.concatenate([blk[1] for blk in blocks], axis=1)
    row_max, row_sum, weighted = state
    score_scale = queries.shape[-1] ** (-0.5)
    scores = (
        jnp.einsum("hqd,hkd->hqk", queries, key_rows, preferred_element_type=jnp.float32)
        * score_scale
    )
    scores = jnp.where(is_live[None, None, :], scores, -jnp.inf)
    new_max = jnp.maximum(row_max, jnp.max(scores, axis=2))
    exps = jnp.exp(scores - new_max[:, :, None])
    decay = jnp.exp(row_max - new_max)
    row_sum = row_sum * decay + jnp.sum(exps, axis=2)
    weighted = weighted * decay[:, :, None] + jnp.einsum(
        "hqk,hkd->hqd", exps.astype(jnp.bfloat16), value_rows, preferred_element_type=jnp.float32
    )
    return (new_max, row_sum, weighted)


def merge_states(first, second):
    max_a, sum_a, acc_a = first
    max_b, sum_b, acc_b = second
    new_max = jnp.maximum(max_a, max_b)
    scale_a = jnp.exp(max_a - new_max)
    scale_b = jnp.exp(max_b - new_max)
    return (
        new_max,
        sum_a * scale_a + sum_b * scale_b,
        acc_a * scale_a[:, :, None] + acc_b * scale_b[:, :, None],
    )


def tp_sum(tree):
    count = lax.axis_size("tp")
    bit = 0
    while 1 << bit < count:
        far = swapped(tree, "tp", bit)
        tree = jax.tree.map(lambda a, b: a + b, tree, far)
        bit += 1
    return tree


def on_device(
    hidden,
    positions,
    lengths,
    step_index,
    layer_mod,
    final_mod,
    qkv_weight,
    q_gain,
    k_gain,
    out_weight,
    final_weight,
    latents,
):
    spread = lax.axis_size("seq") // 4
    bit_count = spread.bit_length() - 1
    seq_pos = lax.axis_index("seq")
    local_seq = seq_pos // spread
    shard_pos = seq_pos % spread
    count_x = spread // 2
    my_x = shard_pos // 2
    my_z = shard_pos % 2
    tp_pos = lax.axis_index("tp")
    local_width = hidden.shape[1]
    tp_count = lax.axis_size("tp")
    parts = [hidden]
    for shift in range(1, tp_count):
        route = [(src, (src + shift) % tp_count) for src in range(tp_count)]
        parts.append(lax.ppermute(hidden, "tp", route))
    stacked = jnp.stack(parts)
    gathered = jnp.concatenate(
        [
            lax.dynamic_index_in_dim(stacked, (tp_pos - owner) % tp_count, 0, keepdims=False)
            for owner in range(tp_count)
        ],
        axis=1,
    )
    model_width = gathered.shape[1]
    rows_dev = gathered.shape[0]
    layer_terms = lax.dynamic_index_in_dim(layer_mod, local_seq, 0, keepdims=False)
    text_count = lax.dynamic_index_in_dim(lengths, local_seq, 0, keepdims=False)
    modulated = modulate(gathered.astype(jnp.float32), layer_terms[0], layer_terms[1]).astype(
        jnp.bfloat16
    )
    head_dim = q_gain.shape[0]
    head_cols = qkv_weight.shape[2]
    heads_here = head_cols // head_dim
    weight4 = qkv_weight.reshape(model_width, 3, heads_here, head_dim)
    projected = jnp.einsum(
        "rf,fchd->chrd", modulated, weight4, preferred_element_type=jnp.float32
    )
    cosine, signed_sine, even = rope_tables(positions)
    queries = rotate(rms_gain(projected[0], q_gain), cosine, signed_sine, even).astype(jnp.bfloat16)
    key_rot = rotate(rms_gain(projected[1], k_gain), cosine, signed_sine, even).astype(jnp.bfloat16)
    values = projected[2].astype(jnp.bfloat16)
    own = jnp.stack([key_rot, values])

    to_left = seq_route(spread, lambda x, z, n: (x - 1, z))
    to_right = seq_route(spread, lambda x, z, n: (x + 1, z))
    to_other_z = seq_route(spread, lambda x, z, n: (x, 1 - z))

    def shard_of(x, z):
        return (x % count_x) * 2 + z

    got_z = lax.ppermute(own, "seq", to_other_z)
    got_right = lax.ppermute(own, "seq", to_left)
    got_left = lax.ppermute(own, "seq", to_right)

    softmax_state = (
        jnp.full((heads_here, rows_dev), -jnp.inf, jnp.float32),
        jnp.zeros((heads_here, rows_dev), jnp.float32),
        jnp.zeros((heads_here, rows_dev, head_dim), jnp.float32),
    )
    softmax_state = fold_block(softmax_state, queries, own[0], own[1], shard_pos, text_count)

    z_from_right, far_keys = lax.ppermute((got_z, got_right[0]), "seq", to_left)
    z_from_left, far_values = lax.ppermute((got_z, got_left[1]), "seq", to_right)

    other_z = 1 - my_z
    softmax_state = fold_group(
        softmax_state,
        queries,
        [
            (got_z[0], got_z[1], shard_of(my_x, other_z)),
            (got_right[0], got_right[1], shard_of(my_x + 1, my_z)),
            (got_left[0], got_left[1], shard_of(my_x - 1, my_z)),
        ],
        text_count,
    )

    far_z_keys = lax.ppermute(z_from_right[0], "seq", to_left)
    far_z_values = lax.ppermute(z_from_left[1], "seq", to_right)

    late_state = (
        jnp.full((heads_here, rows_dev), -jnp.inf, jnp.float32),
        jnp.zeros((heads_here, rows_dev), jnp.float32),
        jnp.zeros((heads_here, rows_dev, head_dim), jnp.float32),
    )
    late_state = fold_group(
        late_state,
        queries,
        [
            (far_keys, far_values, shard_of(my_x + 2, my_z)),
            (z_from_right[0], z_from_right[1], shard_of(my_x + 1, other_z)),
            (z_from_left[0], z_from_left[1], shard_of(my_x - 1, other_z)),
        ],
        text_count,
    )
    softmax_state = fold_block(
        softmax_state, queries, far_z_keys, far_z_values, shard_of(my_x + 2, other_z), text_count
    )
    softmax_state = merge_states(softmax_state, late_state)

    row_max, row_sum, weighted = softmax_state
    attended = (weighted / row_sum[:, :, None]).astype(jnp.bfloat16)
    log_sums = row_max + jnp.log(row_sum)
    hold = jnp.minimum(jnp.abs(queries[0, 0, 0]), 0).astype(out_weight.dtype)
    attended_parts = [attended]
    weight_parts = [lax.dynamic_slice_in_dim(out_weight, tp_pos * local_width, local_width, 1)]
    pair_pos = lax.axis_index("pair")
    assert lax.axis_size("pair") == 2
    half = local_width // 2
    fetched = []
    for shift in range(1, tp_count):
        route = [(src, (src + shift) % tp_count) for src in range(tp_count)]
        dest = (tp_pos + shift) % tp_count
        weight_send = lax.dynamic_slice_in_dim(
            out_weight, dest * local_width + pair_pos * half, half, 1
        )
        fetched.append(lax.ppermute(weight_send + hold, "tp", route))
        attended_parts.append(lax.ppermute(attended, "tp", route))
    fetched = jnp.stack(fetched)
    late = jnp.minimum(jnp.abs(far_z_keys[0, 0, 0]), 0).astype(fetched.dtype)
    other_half = lax.ppermute(fetched + late, "pair", [(0, 1), (1, 0)])
    first_half = jnp.where(pair_pos == 0, fetched, other_half)
    second_half = jnp.where(pair_pos == 0, other_half, fetched)
    joined = jnp.concatenate([first_half, second_half], axis=2)
    weight_parts += [joined[index] for index in range(tp_count - 1)]
    all_attended = jnp.stack(attended_parts)
    all_weights = jnp.stack(weight_parts).reshape(tp_count, heads_here, head_dim, local_width)
    update = jnp.einsum(
        "khrd,khdf->rf", all_attended, all_weights, preferred_element_type=jnp.float32
    )
    gate_slice = lax.dynamic_slice_in_dim(layer_terms[2], tp_pos * local_width, local_width, 0)
    new_hidden = (hidden.astype(jnp.float32) + gate_slice * update).astype(jnp.bfloat16)

    final_terms = lax.dynamic_index_in_dim(final_mod, local_seq, 0, keepdims=False)
    final_shift = lax.dynamic_slice_in_dim(final_terms[0], tp_pos * local_width, local_width, 0)
    final_scale = lax.dynamic_slice_in_dim(final_terms[1], tp_pos * local_width, local_width, 0)
    image_rows = new_hidden[:IMG_DEV].astype(jnp.float32)
    weight = final_weight.astype(jnp.float32)
    scale_one = 1.0 + final_scale
    highest = lax.Precision.HIGHEST
    terms = (
        jnp.sum(image_rows, axis=1),
        jnp.sum(image_rows * image_rows, axis=1),
        jnp.dot(image_rows * scale_one, weight, precision=highest),
        jnp.dot(scale_one[None, :], weight, precision=highest),
        jnp.dot(final_shift[None, :], weight, precision=highest),
    )
    row_sums, squares, scaled_proj, scale_proj, shift_proj = tp_sum(terms)
    row_mean = row_sums / model_width
    inv_std = lax.rsqrt(squares / model_width - row_mean * row_mean + 1e-06)
    velocity = (
        inv_std[:, None] * (scaled_proj - row_mean[:, None] * scale_proj) + shift_proj
    )

    half_rows = IMG_DEV // 2
    is_cond = local_seq % 2 == 0
    outgoing = jnp.where(is_cond, velocity[half_rows:], velocity[:half_rows])
    partner_half = swapped(outgoing, "seq", bit_count)
    own_half = jnp.where(is_cond, velocity[:half_rows], velocity[half_rows:])
    cond_vel = jnp.where(is_cond, own_half, partner_half)
    uncond_vel = jnp.where(is_cond, partner_half, own_half)
    guided = uncond_vel + GUIDE * (cond_vel - uncond_vel)
    step_now = step_index[0]
    time_step = sigma_at(step_now + 1) - sigma_at(step_now)
    return (new_hidden, log_sums, latents + time_step * guided)


def solution(mesh):
    return jax.shard_map(
        on_device,
        mesh=mesh,
        in_specs=(
            P(("pair", "seq"), "tp"),
            P(None, ("pair", "seq")),
            P("pair"),
            P(),
            P("pair", None, None),
            P("pair", None, None),
            P(None, None, "tp"),
            P(),
            P(),
            P("tp", None),
            P("tp", None),
            P(("pair", "seq"), None),
        ),
        out_specs=(P(("pair", "seq"), "tp"), P("tp", ("pair", "seq")), P(("pair", "seq"), None)),
        check_vma=False,
    )
```

```python
import jax
import jax.numpy as jnp
from jax import lax
from jax.sharding import PartitionSpec as P

ROPE_T = 16
ROPE_H = 56
ROPE_W = 56
STEPS = 8
IMG_DEV = 512
TXT_DEV = 64


GUIDE = 3.5
SHIFT = 3.0


def swapped(block, axis, bit):
    count = lax.axis_size(axis)
    route = []
    for low in range(count):
        high = low | 1 << bit
        if high != low and high < count:
            route += [(low, high), (high, low)]
    return lax.ppermute(block, axis, route)


def seq_route(spread, move):
    count_x = spread // 2
    route = []
    for group in range(4):
        for shard in range(spread):
            dest_x, dest_z = move(shard // 2, shard % 2, count_x)
            route.append((group * spread + shard, group * spread + (dest_x % count_x) * 2 + dest_z))
    return route


def rope_tables(ids_block):
    angle_parts = []
    for axis_pos, rope_width in ((0, ROPE_T), (1, ROPE_H), (2, ROPE_W)):
        frequencies = 10000.0 ** (-jnp.arange(0, rope_width, 2).astype(jnp.float32) / rope_width)
        angle_parts.append(ids_block[axis_pos].astype(jnp.float32)[:, None] * frequencies[None, :])
    angles = jnp.concatenate(angle_parts, axis=1)
    angles = jnp.repeat(angles, 2, axis=1)
    even = (jnp.arange(angles.shape[1]) % 2 == 0)[None, :]
    sine = jnp.sin(angles)
    return (jnp.cos(angles), jnp.where(even, -sine, sine), even)


def rotate(tensor, cosine, signed_sine, even):
    partner = jnp.where(
        even[None], jnp.roll(tensor, -1, axis=-1), jnp.roll(tensor, 1, axis=-1)
    )
    return tensor * cosine[None] + partner * signed_sine[None]


def rms_gain(tensor, gain_vec):
    return tensor * lax.rsqrt(jnp.mean(tensor * tensor, axis=-1, keepdims=True) + 1e-06) * gain_vec


def modulate(features, shift_vec, scale_vec):
    row_mean = jnp.mean(features, axis=-1, keepdims=True)
    row_var = jnp.mean(features * features, axis=-1, keepdims=True) - row_mean * row_mean
    return (features - row_mean) * lax.rsqrt(row_var + 1e-06) * (1.0 + scale_vec) + shift_vec


def sigma_at(step_now):
    time_now = 1.0 - step_now.astype(jnp.float32) / STEPS
    return SHIFT * time_now / (1.0 + (SHIFT - 1.0) * time_now)


def fold_block(state, queries, key_block, value_block, shard, text_count):
    row_max, row_sum, weighted = state
    rows_dev = key_block.shape[1]
    offset = jnp.arange(rows_dev, dtype=jnp.int32)
    text_index = shard * TXT_DEV + offset - IMG_DEV
    is_live = (offset < IMG_DEV) | (text_index < text_count)
    score_scale = queries.shape[-1] ** (-0.5)
    scores = (
        jnp.einsum("hqd,hkd->hqk", queries, key_block, preferred_element_type=jnp.float32)
        * score_scale
    )
    scores = jnp.where(is_live[None, None, :], scores, -jnp.inf)
    new_max = jnp.maximum(row_max, jnp.max(scores, axis=2))
    exps = jnp.exp(scores - new_max[:, :, None])
    decay = jnp.exp(row_max - new_max)
    row_sum = row_sum * decay + jnp.sum(exps, axis=2)
    weighted = weighted * decay[:, :, None] + jnp.einsum(
        "hqk,hkd->hqd", exps.astype(jnp.bfloat16), value_block, preferred_element_type=jnp.float32
    )
    return (new_max, row_sum, weighted)


def fold_group(state, queries, blocks, text_count):
    rows = blocks[0][0].shape[1]
    offset = jnp.arange(rows, dtype=jnp.int32)
    is_live = jnp.concatenate(
        [(offset < IMG_DEV) | (shard * TXT_DEV + offset - IMG_DEV < text_count) for _, _, shard in blocks]
    )
    key_rows = jnp.concatenate([blk[0] for blk in blocks], axis=1)
    value_rows = jnp.concatenate([blk[1] for blk in blocks], axis=1)
    row_max, row_sum, weighted = state
    score_scale = queries.shape[-1] ** (-0.5)
    scores = (
        jnp.einsum("hqd,hkd->hqk", queries, key_rows, preferred_element_type=jnp.float32)
        * score_scale
    )
    scores = jnp.where(is_live[None, None, :], scores, -jnp.inf)
    new_max = jnp.maximum(row_max, jnp.max(scores, axis=2))
    exps = jnp.exp(scores - new_max[:, :, None])
    decay = jnp.exp(row_max - new_max)
    row_sum = row_sum * decay + jnp.sum(exps, axis=2)
    weighted = weighted * decay[:, :, None] + jnp.einsum(
        "hqk,hkd->hqd", exps.astype(jnp.bfloat16), value_rows, preferred_element_type=jnp.float32
    )
    return (new_max, row_sum, weighted)


def merge_states(first, second):
    max_a, sum_a, acc_a = first
    max_b, sum_b, acc_b = second
    new_max = jnp.maximum(max_a, max_b)
    scale_a = jnp.exp(max_a - new_max)
    scale_b = jnp.exp(max_b - new_max)
    return (
        new_max,
        sum_a * scale_a + sum_b * scale_b,
        acc_a * scale_a[:, :, None] + acc_b * scale_b[:, :, None],
    )


def tp_sum(tree):
    count = lax.axis_size("tp")
    bit = 0
    while 1 << bit < count:
        far = swapped(tree, "tp", bit)
        tree = jax.tree.map(lambda a, b: a + b, tree, far)
        bit += 1
    return tree


def on_device(
    hidden,
    positions,
    lengths,
    step_index,
    layer_mod,
    final_mod,
    qkv_weight,
    q_gain,
    k_gain,
    out_weight,
    final_weight,
    latents,
):
    spread = lax.axis_size("seq") // 4
    bit_count = spread.bit_length() - 1
    seq_pos = lax.axis_index("seq")
    local_seq = seq_pos // spread
    shard_pos = seq_pos % spread
    count_x = spread // 2
    my_x = shard_pos // 2
    my_z = shard_pos % 2
    tp_pos = lax.axis_index("tp")
    local_width = hidden.shape[1]
    tp_count = lax.axis_size("tp")
    parts = [hidden]
    for shift in range(1, tp_count):
        route = [(src, (src + shift) % tp_count) for src in range(tp_count)]
        parts.append(lax.ppermute(hidden, "tp", route))
    stacked = jnp.stack(parts)
    gathered = jnp.concatenate(
        [
            lax.dynamic_index_in_dim(stacked, (tp_pos - owner) % tp_count, 0, keepdims=False)
            for owner in range(tp_count)
        ],
        axis=1,
    )
    model_width = gathered.shape[1]
    rows_dev = gathered.shape[0]
    layer_terms = lax.dynamic_index_in_dim(layer_mod, local_seq, 0, keepdims=False)
    text_count = lax.dynamic_index_in_dim(lengths, local_seq, 0, keepdims=False)
    modulated = modulate(gathered.astype(jnp.float32), layer_terms[0], layer_terms[1]).astype(
        jnp.bfloat16
    )
    head_dim = q_gain.shape[0]
    head_cols = qkv_weight.shape[2]
    heads_here = head_cols // head_dim
    weight4 = qkv_weight.reshape(model_width, 3, heads_here, head_dim)
    projected = jnp.einsum(
        "rf,fchd->chrd", modulated, weight4, preferred_element_type=jnp.float32
    )
    cosine, signed_sine, even = rope_tables(positions)
    queries = rotate(rms_gain(projected[0], q_gain), cosine, signed_sine, even).astype(jnp.bfloat16)
    key_rot = rotate(rms_gain(projected[1], k_gain), cosine, signed_sine, even).astype(jnp.bfloat16)
    values = projected[2].astype(jnp.bfloat16)
    own = jnp.stack([key_rot, values])

    to_left = seq_route(spread, lambda x, z, n: (x - 1, z))
    to_right = seq_route(spread, lambda x, z, n: (x + 1, z))
    to_other_z = seq_route(spread, lambda x, z, n: (x, 1 - z))

    def shard_of(x, z):
        return (x % count_x) * 2 + z

    got_z = lax.ppermute(own, "seq", to_other_z)
    got_right = lax.ppermute(own, "seq", to_left)
    got_left = lax.ppermute(own, "seq", to_right)

    softmax_state = (
        jnp.full((heads_here, rows_dev), -jnp.inf, jnp.float32),
        jnp.zeros((heads_here, rows_dev), jnp.float32),
        jnp.zeros((heads_here, rows_dev, head_dim), jnp.float32),
    )
    softmax_state = fold_block(softmax_state, queries, own[0], own[1], shard_pos, text_count)

    z_from_right, far_keys = lax.ppermute((got_z, got_right[0]), "seq", to_left)
    z_from_left, far_values = lax.ppermute((got_z, got_left[1]), "seq", to_right)

    other_z = 1 - my_z
    softmax_state = fold_group(
        softmax_state,
        queries,
        [
            (got_z[0], got_z[1], shard_of(my_x, other_z)),
            (got_right[0], got_right[1], shard_of(my_x + 1, my_z)),
            (got_left[0], got_left[1], shard_of(my_x - 1, my_z)),
        ],
        text_count,
    )

    far_z_keys = lax.ppermute(z_from_right[0], "seq", to_left)
    far_z_values = lax.ppermute(z_from_left[1], "seq", to_right)

    softmax_state = fold_group(
        softmax_state,
        queries,
        [
            (far_keys, far_values, shard_of(my_x + 2, my_z)),
            (z_from_right[0], z_from_right[1], shard_of(my_x + 1, other_z)),
            (z_from_left[0], z_from_left[1], shard_of(my_x - 1, other_z)),
        ],
        text_count,
    )
    softmax_state = fold_block(
        softmax_state, queries, far_z_keys, far_z_values, shard_of(my_x + 2, other_z), text_count
    )

    row_max, row_sum, weighted = softmax_state
    attended = (weighted / row_sum[:, :, None]).astype(jnp.bfloat16)
    log_sums = row_max + jnp.log(row_sum)
    hold = jnp.minimum(jnp.abs(queries[0, 0, 0]), 0).astype(out_weight.dtype)
    attended_parts = [attended]
    weight_parts = [lax.dynamic_slice_in_dim(out_weight, tp_pos * local_width, local_width, 1)]
    for shift in range(1, tp_count):
        route = [(src, (src + shift) % tp_count) for src in range(tp_count)]
        dest = (tp_pos + shift) % tp_count
        weight_send = lax.dynamic_slice_in_dim(out_weight, dest * local_width, local_width, 1)
        weight_parts.append(lax.ppermute(weight_send + hold, "tp", route))
        attended_parts.append(lax.ppermute(attended, "tp", route))
    all_attended = jnp.stack(attended_parts)
    all_weights = jnp.stack(weight_parts).reshape(tp_count, heads_here, head_dim, local_width)
    update = jnp.einsum(
        "khrd,khdf->rf", all_attended, all_weights, preferred_element_type=jnp.float32
    )
    gate_slice = lax.dynamic_slice_in_dim(layer_terms[2], tp_pos * local_width, local_width, 0)
    new_hidden = (hidden.astype(jnp.float32) + gate_slice * update).astype(jnp.bfloat16)

    final_terms = lax.dynamic_index_in_dim(final_mod, local_seq, 0, keepdims=False)
    final_shift = lax.dynamic_slice_in_dim(final_terms[0], tp_pos * local_width, local_width, 0)
    final_scale = lax.dynamic_slice_in_dim(final_terms[1], tp_pos * local_width, local_width, 0)
    image_rows = new_hidden[:IMG_DEV].astype(jnp.float32)
    weight = final_weight.astype(jnp.float32)
    scale_one = 1.0 + final_scale
    highest = lax.Precision.HIGHEST
    terms = (
        jnp.sum(image_rows, axis=1),
        jnp.sum(image_rows * image_rows, axis=1),
        jnp.dot(image_rows * scale_one, weight, precision=highest),
        jnp.dot(scale_one[None, :], weight, precision=highest),
        jnp.dot(final_shift[None, :], weight, precision=highest),
    )
    row_sums, squares, scaled_proj, scale_proj, shift_proj = tp_sum(terms)
    row_mean = row_sums / model_width
    inv_std = lax.rsqrt(squares / model_width - row_mean * row_mean + 1e-06)
    velocity = (
        inv_std[:, None] * (scaled_proj - row_mean[:, None] * scale_proj) + shift_proj
    )

    half_rows = IMG_DEV // 2
    is_cond = local_seq % 2 == 0
    outgoing = jnp.where(is_cond, velocity[half_rows:], velocity[:half_rows])
    partner_half = swapped(outgoing, "seq", bit_count)
    own_half = jnp.where(is_cond, velocity[:half_rows], velocity[half_rows:])
    cond_vel = jnp.where(is_cond, own_half, partner_half)
    uncond_vel = jnp.where(is_cond, partner_half, own_half)
    guided = uncond_vel + GUIDE * (cond_vel - uncond_vel)
    step_now = step_index[0]
    time_step = sigma_at(step_now + 1) - sigma_at(step_now)
    return (new_hidden, log_sums, latents + time_step * guided)


def solution(mesh):
    return jax.shard_map(
        on_device,
        mesh=mesh,
        in_specs=(
            P(("pair", "seq"), "tp"),
            P(None, ("pair", "seq")),
            P("pair"),
            P(),
            P("pair", None, None),
            P("pair", None, None),
            P(None, None, "tp"),
            P(),
            P(),
            P("tp", None),
            P("tp", None),
            P(("pair", "seq"), None),
        ),
        out_specs=(P(("pair", "seq"), "tp"), P("tp", ("pair", "seq")), P(("pair", "seq"), None)),
        check_vma=False,
    )
```

```python
import jax
import jax.numpy as jnp
from jax import lax
from jax.sharding import PartitionSpec as P

ROPE_T = 16
ROPE_H = 56
ROPE_W = 56
STEPS = 8
IMG_DEV = 512
TXT_DEV = 64


GUIDE = 3.5
SHIFT = 3.0


def swapped(block, axis, bit):
    count = lax.axis_size(axis)
    route = []
    for low in range(count):
        high = low | 1 << bit
        if high != low and high < count:
            route += [(low, high), (high, low)]
    return lax.ppermute(block, axis, route)


def seq_route(spread, move):
    count_x = spread // 2
    route = []
    for group in range(4):
        for shard in range(spread):
            dest_x, dest_z = move(shard // 2, shard % 2, count_x)
            route.append((group * spread + shard, group * spread + (dest_x % count_x) * 2 + dest_z))
    return route


def rope_tables(ids_block):
    angle_parts = []
    for axis_pos, rope_width in ((0, ROPE_T), (1, ROPE_H), (2, ROPE_W)):
        frequencies = 10000.0 ** (-jnp.arange(0, rope_width, 2).astype(jnp.float32) / rope_width)
        angle_parts.append(ids_block[axis_pos].astype(jnp.float32)[:, None] * frequencies[None, :])
    angles = jnp.concatenate(angle_parts, axis=1)
    angles = jnp.repeat(angles, 2, axis=1)
    even = (jnp.arange(angles.shape[1]) % 2 == 0)[None, :]
    sine = jnp.sin(angles)
    return (jnp.cos(angles), jnp.where(even, -sine, sine), even)


def rotate(tensor, cosine, signed_sine, even):
    partner = jnp.where(
        even[None], jnp.roll(tensor, -1, axis=-1), jnp.roll(tensor, 1, axis=-1)
    )
    return tensor * cosine[None] + partner * signed_sine[None]


def rms_gain(tensor, gain_vec):
    return tensor * lax.rsqrt(jnp.mean(tensor * tensor, axis=-1, keepdims=True) + 1e-06) * gain_vec


def modulate(features, shift_vec, scale_vec):
    row_mean = jnp.mean(features, axis=-1, keepdims=True)
    row_var = jnp.mean(features * features, axis=-1, keepdims=True) - row_mean * row_mean
    return (features - row_mean) * lax.rsqrt(row_var + 1e-06) * (1.0 + scale_vec) + shift_vec


def sigma_at(step_now):
    time_now = 1.0 - step_now.astype(jnp.float32) / STEPS
    return SHIFT * time_now / (1.0 + (SHIFT - 1.0) * time_now)


def fold_block(state, queries, key_block, value_block, shard, text_count):
    row_max, row_sum, weighted = state
    rows_dev = key_block.shape[1]
    offset = jnp.arange(rows_dev, dtype=jnp.int32)
    text_index = shard * TXT_DEV + offset - IMG_DEV
    is_live = (offset < IMG_DEV) | (text_index < text_count)
    score_scale = queries.shape[-1] ** (-0.5)
    scores = (
        jnp.einsum("hqd,hkd->hqk", queries, key_block, preferred_element_type=jnp.float32)
        * score_scale
    )
    scores = jnp.where(is_live[None, None, :], scores, -jnp.inf)
    new_max = jnp.maximum(row_max, jnp.max(scores, axis=2))
    exps = jnp.exp(scores - new_max[:, :, None])
    decay = jnp.exp(row_max - new_max)
    row_sum = row_sum * decay + jnp.sum(exps, axis=2)
    weighted = weighted * decay[:, :, None] + jnp.einsum(
        "hqk,hkd->hqd", exps.astype(jnp.bfloat16), value_block, preferred_element_type=jnp.float32
    )
    return (new_max, row_sum, weighted)


def fold_group(state, queries, blocks, text_count):
    rows = blocks[0][0].shape[1]
    offset = jnp.arange(rows, dtype=jnp.int32)
    is_live = jnp.concatenate(
        [(offset < IMG_DEV) | (shard * TXT_DEV + offset - IMG_DEV < text_count) for _, _, shard in blocks]
    )
    key_rows = jnp.concatenate([blk[0] for blk in blocks], axis=1)
    value_rows = jnp.concatenate([blk[1] for blk in blocks], axis=1)
    row_max, row_sum, weighted = state
    score_scale = queries.shape[-1] ** (-0.5)
    scores = (
        jnp.einsum("hqd,hkd->hqk", queries, key_rows, preferred_element_type=jnp.float32)
        * score_scale
    )
    scores = jnp.where(is_live[None, None, :], scores, -jnp.inf)
    new_max = jnp.maximum(row_max, jnp.max(scores, axis=2))
    exps = jnp.exp(scores - new_max[:, :, None])
    decay = jnp.exp(row_max - new_max)
    row_sum = row_sum * decay + jnp.sum(exps, axis=2)
    weighted = weighted * decay[:, :, None] + jnp.einsum(
        "hqk,hkd->hqd", exps.astype(jnp.bfloat16), value_rows, preferred_element_type=jnp.float32
    )
    return (new_max, row_sum, weighted)


def merge_states(first, second):
    max_a, sum_a, acc_a = first
    max_b, sum_b, acc_b = second
    new_max = jnp.maximum(max_a, max_b)
    scale_a = jnp.exp(max_a - new_max)
    scale_b = jnp.exp(max_b - new_max)
    return (
        new_max,
        sum_a * scale_a + sum_b * scale_b,
        acc_a * scale_a[:, :, None] + acc_b * scale_b[:, :, None],
    )


def tp_sum(tree):
    count = lax.axis_size("tp")
    bit = 0
    while 1 << bit < count:
        far = swapped(tree, "tp", bit)
        tree = jax.tree.map(lambda a, b: a + b, tree, far)
        bit += 1
    return tree


def on_device(
    hidden,
    positions,
    lengths,
    step_index,
    layer_mod,
    final_mod,
    qkv_weight,
    q_gain,
    k_gain,
    out_weight,
    final_weight,
    latents,
):
    spread = lax.axis_size("seq") // 4
    bit_count = spread.bit_length() - 1
    seq_pos = lax.axis_index("seq")
    local_seq = seq_pos // spread
    shard_pos = seq_pos % spread
    count_x = spread // 2
    my_x = shard_pos // 2
    my_z = shard_pos % 2
    tp_pos = lax.axis_index("tp")
    local_width = hidden.shape[1]
    tp_count = lax.axis_size("tp")
    parts = [hidden]
    for shift in range(1, tp_count):
        route = [(src, (src + shift) % tp_count) for src in range(tp_count)]
        parts.append(lax.ppermute(hidden, "tp", route))
    stacked = jnp.stack(parts)
    gathered = jnp.concatenate(
        [
            lax.dynamic_index_in_dim(stacked, (tp_pos - owner) % tp_count, 0, keepdims=False)
            for owner in range(tp_count)
        ],
        axis=1,
    )
    model_width = gathered.shape[1]
    rows_dev = gathered.shape[0]
    layer_terms = lax.dynamic_index_in_dim(layer_mod, local_seq, 0, keepdims=False)
    text_count = lax.dynamic_index_in_dim(lengths, local_seq, 0, keepdims=False)
    modulated = modulate(gathered.astype(jnp.float32), layer_terms[0], layer_terms[1]).astype(
        jnp.bfloat16
    )
    head_dim = q_gain.shape[0]
    head_cols = qkv_weight.shape[2]
    heads_here = head_cols // head_dim
    weight4 = qkv_weight.reshape(model_width, 3, heads_here, head_dim)
    projected = jnp.einsum(
        "rf,fchd->chrd", modulated, weight4[:, 1:], preferred_element_type=jnp.float32
    )
    cosine, signed_sine, even = rope_tables(positions)
    key_rot = rotate(rms_gain(projected[0], k_gain), cosine, signed_sine, even).astype(jnp.bfloat16)
    values = projected[1].astype(jnp.bfloat16)
    query_proj = jnp.einsum(
        "rf,fhd->hrd", modulated, weight4[:, 0], preferred_element_type=jnp.float32
    )
    queries = rotate(rms_gain(query_proj, q_gain), cosine, signed_sine, even).astype(jnp.bfloat16)
    own = jnp.stack([key_rot, values])

    to_left = seq_route(spread, lambda x, z, n: (x - 1, z))
    to_right = seq_route(spread, lambda x, z, n: (x + 1, z))
    to_other_z = seq_route(spread, lambda x, z, n: (x, 1 - z))

    def shard_of(x, z):
        return (x % count_x) * 2 + z

    got_z = lax.ppermute(own, "seq", to_other_z)
    got_right = lax.ppermute(own, "seq", to_left)
    got_left = lax.ppermute(own, "seq", to_right)

    softmax_state = (
        jnp.full((heads_here, rows_dev), -jnp.inf, jnp.float32),
        jnp.zeros((heads_here, rows_dev), jnp.float32),
        jnp.zeros((heads_here, rows_dev, head_dim), jnp.float32),
    )
    softmax_state = fold_block(softmax_state, queries, own[0], own[1], shard_pos, text_count)

    z_from_right, far_keys = lax.ppermute((got_z, got_right[0]), "seq", to_left)
    z_from_left, far_values = lax.ppermute((got_z, got_left[1]), "seq", to_right)

    other_z = 1 - my_z
    softmax_state = fold_group(
        softmax_state,
        queries,
        [
            (got_z[0], got_z[1], shard_of(my_x, other_z)),
            (got_right[0], got_right[1], shard_of(my_x + 1, my_z)),
            (got_left[0], got_left[1], shard_of(my_x - 1, my_z)),
        ],
        text_count,
    )

    far_z_keys = lax.ppermute(z_from_right[0], "seq", to_left)
    far_z_values = lax.ppermute(z_from_left[1], "seq", to_right)

    late_state = (
        jnp.full((heads_here, rows_dev), -jnp.inf, jnp.float32),
        jnp.zeros((heads_here, rows_dev), jnp.float32),
        jnp.zeros((heads_here, rows_dev, head_dim), jnp.float32),
    )
    late_state = fold_group(
        late_state,
        queries,
        [
            (far_keys, far_values, shard_of(my_x + 2, my_z)),
            (z_from_right[0], z_from_right[1], shard_of(my_x + 1, other_z)),
            (z_from_left[0], z_from_left[1], shard_of(my_x - 1, other_z)),
        ],
        text_count,
    )
    softmax_state = fold_block(
        softmax_state, queries, far_z_keys, far_z_values, shard_of(my_x + 2, other_z), text_count
    )
    softmax_state = merge_states(softmax_state, late_state)

    row_max, row_sum, weighted = softmax_state
    attended = (weighted / row_sum[:, :, None]).astype(jnp.bfloat16)
    log_sums = row_max + jnp.log(row_sum)
    hold = jnp.minimum(jnp.abs(queries[0, 0, 0]), 0).astype(out_weight.dtype)
    attended_parts = [attended]
    weight_parts = [lax.dynamic_slice_in_dim(out_weight, tp_pos * local_width, local_width, 1)]
    for shift in range(1, tp_count):
        route = [(src, (src + shift) % tp_count) for src in range(tp_count)]
        dest = (tp_pos + shift) % tp_count
        weight_send = lax.dynamic_slice_in_dim(out_weight, dest * local_width, local_width, 1)
        weight_parts.append(lax.ppermute(weight_send + hold, "tp", route))
        attended_parts.append(lax.ppermute(attended, "tp", route))
    all_attended = jnp.stack(attended_parts)
    all_weights = jnp.stack(weight_parts).reshape(tp_count, heads_here, head_dim, local_width)
    update = jnp.einsum(
        "khrd,khdf->rf", all_attended, all_weights, preferred_element_type=jnp.float32
    )
    gate_slice = lax.dynamic_slice_in_dim(layer_terms[2], tp_pos * local_width, local_width, 0)
    new_hidden = (hidden.astype(jnp.float32) + gate_slice * update).astype(jnp.bfloat16)

    final_terms = lax.dynamic_index_in_dim(final_mod, local_seq, 0, keepdims=False)
    final_shift = lax.dynamic_slice_in_dim(final_terms[0], tp_pos * local_width, local_width, 0)
    final_scale = lax.dynamic_slice_in_dim(final_terms[1], tp_pos * local_width, local_width, 0)
    image_rows = new_hidden[:IMG_DEV].astype(jnp.float32)
    weight = final_weight.astype(jnp.float32)
    scale_one = 1.0 + final_scale
    highest = lax.Precision.HIGHEST
    terms = (
        jnp.sum(image_rows, axis=1),
        jnp.sum(image_rows * image_rows, axis=1),
        jnp.dot(image_rows * scale_one, weight, precision=highest),
        jnp.dot(scale_one[None, :], weight, precision=highest),
        jnp.dot(final_shift[None, :], weight, precision=highest),
    )
    row_sums, squares, scaled_proj, scale_proj, shift_proj = tp_sum(terms)
    row_mean = row_sums / model_width
    inv_std = lax.rsqrt(squares / model_width - row_mean * row_mean + 1e-06)
    velocity = (
        inv_std[:, None] * (scaled_proj - row_mean[:, None] * scale_proj) + shift_proj
    )

    half_rows = IMG_DEV // 2
    is_cond = local_seq % 2 == 0
    outgoing = jnp.where(is_cond, velocity[half_rows:], velocity[:half_rows])
    partner_half = swapped(outgoing, "seq", bit_count)
    own_half = jnp.where(is_cond, velocity[:half_rows], velocity[half_rows:])
    cond_vel = jnp.where(is_cond, own_half, partner_half)
    uncond_vel = jnp.where(is_cond, partner_half, own_half)
    guided = uncond_vel + GUIDE * (cond_vel - uncond_vel)
    step_now = step_index[0]
    time_step = sigma_at(step_now + 1) - sigma_at(step_now)
    return (new_hidden, log_sums, latents + time_step * guided)


def solution(mesh):
    return jax.shard_map(
        on_device,
        mesh=mesh,
        in_specs=(
            P(("pair", "seq"), "tp"),
            P(None, ("pair", "seq")),
            P("pair"),
            P(),
            P("pair", None, None),
            P("pair", None, None),
            P(None, None, "tp"),
            P(),
            P(),
            P("tp", None),
            P("tp", None),
            P(("pair", "seq"), None),
        ),
        out_specs=(P(("pair", "seq"), "tp"), P("tp", ("pair", "seq")), P(("pair", "seq"), None)),
        check_vma=False,
    )
```
